128 devices in a mesh: dp: 4 (over y), exp: 32 (over z, x, core).
Axes of the slice: x: 4, y: 4, z: 4, core: 2. Of those that a mesh axis runs over, the one named last changes fastest.
Arguments:
- hidden: bfloat16 [16384, 2048], P(('dp', 'exp')), may hold values from -6 to 6
- queries: bfloat16 [16384, 2048], P(('dp', 'exp')), may hold values from -1000 to 1000
- draft_entries: bfloat16 [2, 16384, 512], P(None, ('dp', 'exp')), may hold values from -6 to 6
- key_pool: bfloat16 [1024, 64, 512], P(('dp', 'exp')), may hold values from -8 to 8
- value_pool: bfloat16 [1024, 64, 512], P(('dp', 'exp')), may hold values from -6 to 6
- page_table: int32 [256, 4], P(('dp', 'exp')), may hold values from 0 to 31, as said below
- cache_len: int32 [256], P(('dp', 'exp')), may hold values from 2 to 256, as said below
- parents: int32 [256, 64], P(('dp', 'exp')), may hold values from -1 to 62, as said below
- out_proj: bfloat16 [2048, 2048], replicated, may hold values from -0.125 to 0.125
- norm_gain: bfloat16 [2048], replicated, may hold values from 0.099609375 to 1.8984375
- expert_gate: bfloat16 [64, 1408, 2048], P('exp', 'dp'), may hold values from -0.125 to 0.125
- expert_up: bfloat16 [64, 1408, 2048], P('exp', 'dp'), may hold values from -0.125 to 0.125
- expert_down: bfloat16 [64, 1408, 2048], P('exp', 'dp'), may hold values from -0.15625 to 0.15625
- shared_gate: bfloat16 [1408, 2048], P('dp'), may hold values from -0.125 to 0.125
- shared_up: bfloat16 [1408, 2048], P('dp'), may hold values from -0.125 to 0.125
- shared_down: bfloat16 [1408, 2048], P('dp'), may hold values from -0.15625 to 0.15625
- expert_ids: int32 [16384, 6], P(('dp', 'exp')), may hold values from 0 to 63, all different within a row; in each aligned block of 128 rows (0 to 127, 128 to 255, ...) at most 16 rows name the same one
- expert_weights: float32 [16384, 6], P(('dp', 'exp')), may hold values from 0.05 to 0.5
Outputs:
- verified: bfloat16 [16384, 2048], P(('dp', 'exp'))
The draws below stay inside these ranges and needn't reach their ends.
Inputs may be any that keep to these rules, and one draw needn't show every extreme that they name: `page_table`: page ids count within the 4 devices that share the request's index of exp: page q lies on the one of dp index q // 8, as its page q % 8; the requests of those devices together use each of their 32 pages exactly once. `cache_len`: some request has exactly 256 cached positions. parents[r, i] is -1 or an earlier node i' < i of the same request; parents[r, 0] = -1. `expert_ids`: each row names 6 different experts; the 128 rows of one device name one expert at most 16 times, a bound that some block reaches.
All inputs are finite; a program needn't handle non-finite values.
Results may differ from the reference program's by a relative error of at most 0.015.
Values may be sent and summed in bfloat16 or wider, within the bound.
No kernel may reach another device: no remote copies, remote signals or barrier semaphores. Data moves between devices by JAX's collectives and lax.ppermute only.
A program may use at most 192 MiB of HBM per device.

```python
import math
import jax
import jax.numpy as jnp
import numpy as np
from jax import lax

D = 2048
HEADS = 16
KVH = 4
HD = 128
EXPERTS = 64
FF = 1408
TOP = 6
SHFF = 1408
REQ_DEV = 2
DRAFT = 64
PAGE = 64
MAXPG = 4
CAP = 16
DP_SPAN = 4
EXP_SPAN = 32
REQUESTS = 256
TOKENS = 16384
TOK_DEV = 128
POOL = 8
GROUP_PAGES = 32
PAGES = 1024
CMAX = 256
QW = 2048
KW = 512
FF_PART = 352
SH_PART = 352


def group_pages(key):
    ordered = jnp.tile(jnp.arange(GROUP_PAGES, dtype=jnp.int32)[None, :], (EXP_SPAN, 1))
    mixed = jax.random.permutation(jax.random.fold_in(key, 7), ordered, axis=1, independent=True)
    mixed = mixed.reshape(EXP_SPAN, DP_SPAN, REQ_DEV, MAXPG)
    return jnp.transpose(mixed, (1, 0, 2, 3)).reshape(REQUESTS, MAXPG).astype(jnp.int32)


def pool_first(key):
    return jax.random.normal(jax.random.fold_in(key, 11), (PAGES, 1, KW), jnp.float32)


def draw_page_table(key, part):
    return group_pages(key)


def draw_key_pool(key, part):
    opening_keys = pool_first(key)
    remaining = jax.random.normal(jax.random.fold_in(key, 14), (PAGES, PAGE - 1, KW), jnp.float32)
    return jnp.concatenate([opening_keys, remaining], axis=1).astype(jnp.bfloat16)


def draw_queries(key, part):
    values = jax.random.normal(jax.random.fold_in(key, 13), (TOKENS, QW), jnp.float32)
    return values.astype(jnp.bfloat16)


def draw_cache_len(key, part):
    lengths = jax.random.randint(jax.random.fold_in(key, 21), (REQUESTS,), 2, CMAX + 1)
    longest = jax.random.randint(jax.random.fold_in(key, 22), (), 0, REQUESTS)
    return jnp.where(jnp.arange(REQUESTS) == longest, CMAX, lengths).astype(jnp.int32)


def draw_parents(key, part):
    raw_bits = jax.random.randint(jax.random.fold_in(key, 31), (REQUESTS, DRAFT), 0, 1 << 20)
    node_index = jnp.arange(DRAFT, dtype=jnp.int32)
    linked = raw_bits % (node_index + 1)[None, :] - 1
    forced = (jnp.arange(REQUESTS)[:, None] == 0) & (node_index[None, :] == DRAFT - 1)
    return jnp.where(forced, DRAFT - 2, linked).astype(jnp.int32)


def level_of(rng, shape, pieces, least, top_value):
    factor_of, own = 1.0, jax.random.fold_in(rng, 6)
    for position, blocks in pieces:
        heights = jnp.exp(jax.random.uniform(jax.random.fold_in(own, position), (blocks,), jnp.float32, least / len(pieces), top_value / len(pieces)))
        factor_of = factor_of * jnp.repeat(heights, shape[position] // blocks).reshape([-1 if axis == position else 1 for axis in range(len(shape))])
    return factor_of


def deal_out(rng, own, number, rows, number_of, top, reach, slope):
    ranking = jax.random.permutation(rng, number_of)
    heavy_load, ordinary = load_shares(number_of, rows * top, reach, slope, True), load_shares(number_of, rows * top, reach, slope, False)
    places = jnp.arange(number_of)

    def named(tallies, offset_by):
        used = int((tallies > 0).sum())
        fixed = max(1, used // 4)
        passed = fixed + (places - fixed + offset_by * (used - fixed)) % max(1, number_of - fixed)
        return jnp.zeros((number_of,), jnp.int32).at[ranking[jnp.where(places < fixed, places, passed)]].set(jnp.asarray(tallies, jnp.int32))

    tallies = jnp.where(number % 4 == 0, named(heavy_load, number // 4), named(ordinary, number - number // 4 - 1))
    mixed = jax.random.permutation(jax.random.fold_in(own, 3), number_of)
    giver, taker = mixed[0:number_of // 2 * 2:2], mixed[1:number_of // 2 * 2:2]
    room = jnp.minimum(tallies[giver] - 1, reach - tallies[taker]) // 2
    room = jnp.where((giver == ranking[0]) | (taker == ranking[0]) | (tallies[taker] == 0), 0, jnp.maximum(room, 0))
    passed = jax.random.randint(jax.random.fold_in(own, 4), (number_of // 2,), 0, 1 << 20) % (room + 1)
    tallies = tallies.at[giver].add(-passed).at[taker].add(passed)
    members = jnp.searchsorted(jnp.cumsum(tallies), jnp.arange(rows * top), side="right").astype(jnp.int32)
    grid = members.reshape(top, rows).T
    grid = grid[jax.random.permutation(jax.random.fold_in(own, 1), rows)]
    offset_by = jax.random.randint(jax.random.fold_in(own, 2), (rows, 1), 0, top)
    return jnp.take_along_axis(grid, (jnp.arange(top)[None, :] + offset_by) % top, axis=1)


def load_shares(count, total, most, lean, full):
    weights = [(1 << 20) // math.isqrt(standing ** lean) + 1 for standing in range(1, count + 1)]
    largest = most if full else min(most, max(-(-total // count), total * weights[0] // sum(weights)))
    least = 1 if total - largest >= count - 1 else 0
    given, rest = [largest] + [least] * (count - 1), total - largest - least * (count - 1)
    while rest > 0:
        free = [i for i in range(1, count) if given[i] < largest] or [i for i in range(1, count) if given[i] < most]
        mass, left = sum([weights[i] for i in free]), rest
        for i in free:
            more = min(most - given[i], max(1, left * weights[i] // mass), rest)
            given[i] = given[i] + more
            rest = rest - more
    return np.array(given)


def scatter_about(rng, shape, scale, bound, pieces=(), kind=jnp.bfloat16):
    entries = scale * jax.random.normal(rng, shape, jnp.float32)
    if pieces:
        entries = entries * level_of(rng, shape, pieces, -0.22, 0.18)
    return jnp.clip(entries, -bound, bound).astype(kind)


def setup_inputs(seed: int = 0) -> dict:
    key_list = jax.random.split(jax.random.key(seed), 19)
    hidden = scatter_about(key_list[0], (TOKENS, D), 1.0, 6.0, ((0, 128),))
    queries = draw_queries(jax.random.fold_in(key_list[18], 71), 0)
    draft_entries = scatter_about(key_list[2], (2, TOKENS, KW), 1.0, 6.0, ((1, 128),))
    key_pool = draw_key_pool(jax.random.fold_in(key_list[18], 71), 0)
    value_pool = scatter_about(key_list[4], (PAGES, PAGE, KW), 1.0, 6.0, ((0, 128),))
    page_table = draw_page_table(jax.random.fold_in(key_list[18], 71), 0)
    cache_len = draw_cache_len(jax.random.fold_in(key_list[18], 71), 0)
    parents = draw_parents(jax.random.fold_in(key_list[18], 71), 0)
    out_proj = scatter_about(key_list[8], (QW, D), QW ** -0.5, 0.125)
    norm_gain = jnp.clip(1.0 + 0.18 * jax.random.normal(key_list[9], (D,), jnp.float32), 0.099609375, 1.8984375).astype(jnp.bfloat16)
    expert_gate = scatter_about(key_list[10], (EXPERTS, FF, D), D ** -0.5, 0.125, ((0, 32), (1, 4)))
    expert_up = scatter_about(key_list[11], (EXPERTS, FF, D), D ** -0.5, 0.125, ((0, 32), (1, 4)))
    expert_down = scatter_about(key_list[12], (EXPERTS, FF, D), FF ** -0.5, 0.15625, ((0, 32), (1, 4)))
    shared_gate = scatter_about(key_list[13], (SHFF, D), D ** -0.5, 0.125, ((0, 4),))
    shared_up = scatter_about(key_list[14], (SHFF, D), D ** -0.5, 0.125, ((0, 4),))
    shared_down = scatter_about(key_list[15], (SHFF, D), SHFF ** -0.5, 0.15625, ((0, 4),))
    expert_ids_keys = jax.random.split(jax.random.fold_in(key_list[16], 1), TOKENS // TOK_DEV)
    expert_ids_turns = jax.random.permutation(jax.random.fold_in(key_list[16], 3), TOKENS // TOK_DEV)
    expert_ids = jax.vmap(lambda own, number: deal_out(jax.random.fold_in(key_list[16], 2), own, number, TOK_DEV, EXPERTS, TOP, CAP, 2))(expert_ids_keys, expert_ids_turns).reshape((TOKENS, TOP))
    expert_weights = jnp.clip(jnp.exp(math.log(0.5) - 2.3025851 * jax.random.uniform(key_list[17], (TOKENS, TOP), jnp.float32) ** level_of(key_list[17], (TOKENS, TOP), ((0, 128),), -0.2, 0.2)), 0.05, 0.5)
    return {"hidden": hidden, "queries": queries, "draft_entries": draft_entries, "key_pool": key_pool, "value_pool": value_pool, "page_table": page_table, "cache_len": cache_len, "parents": parents, "out_proj": out_proj, "norm_gain": norm_gain, "expert_gate": expert_gate, "expert_up": expert_up, "expert_down": expert_down, "shared_gate": shared_gate, "shared_up": shared_up, "shared_down": shared_down, "expert_ids": expert_ids, "expert_weights": expert_weights}


NEG_FILL = -1e+30
NORM_EPSILON = 1e-06
HIGHEST_PRECISION = lax.Precision.HIGHEST

def tree_reach(parents):
    node_count = parents.shape[-1]
    node_index = jnp.arange(node_count, dtype=jnp.int32)
    linked = (parents[:, :, None] == node_index[None, None, :]).astype(jnp.float32)
    reached = jnp.minimum(linked + jnp.eye(node_count, dtype=jnp.float32)[None], 1.0)
    for rounds in range(max(1, (node_count - 1).bit_length())):
        reached = jnp.minimum(jnp.einsum('rij,rjk->rik', reached, reached, precision=HIGHEST_PRECISION), 1.0)
    return reached

def reference(hidden, queries, draft_entries, key_pool, value_pool, page_table, cache_len, parents, out_proj, norm_gain, expert_gate, expert_up, expert_down, shared_gate, shared_up, shared_down, expert_ids, expert_weights):
    group_size = HEADS // KVH
    reached = tree_reach(parents)
    request_index = jnp.arange(REQUESTS, dtype=jnp.int32)
    columns = request_index // REQ_DEV % EXP_SPAN
    page_index = page_table // POOL * (EXP_SPAN * POOL) + columns[:, None] * POOL + page_table % POOL
    positions = jnp.arange(CMAX, dtype=jnp.int32)

    def attend(items):
        query_rows, draft_keys, draft_values, page_rows, cache_size, reach_rows = items
        cache_keys = key_pool[page_rows].reshape(CMAX, KW)
        cache_values = value_pool[page_rows].reshape(CMAX, KW)
        all_keys = jnp.concatenate([cache_keys, draft_keys], axis=0).astype(jnp.float32).reshape(CMAX + DRAFT, KVH, HD)
        all_values = jnp.concatenate([cache_values, draft_values], axis=0).astype(jnp.float32).reshape(CMAX + DRAFT, KVH, HD)
        query_heads = query_rows.astype(jnp.float32).reshape(DRAFT, KVH, group_size, HD)
        scores = jnp.einsum('tgnd,cgd->gntc', query_heads, all_keys) * HD ** (-0.5)
        cache_live = jnp.broadcast_to(positions[None, :] < cache_size, (DRAFT, CMAX))
        live_mask = jnp.concatenate([cache_live, reach_rows > 0.5], axis=1)
        scores = jnp.where(live_mask[None, None], scores, NEG_FILL)
        row_top = lax.optimization_barrier(jnp.max(scores, axis=-1, keepdims=True))
        exponents = jnp.where(live_mask[None, None], jnp.exp(scores - row_top), 0.0)
        totals = lax.optimization_barrier(jnp.sum(exponents, axis=-1))
        weights = lax.optimization_barrier(exponents.astype(jnp.bfloat16)).astype(jnp.float32)
        mixed = jnp.einsum('gntc,cgd->tgnd', weights, all_values)
        mixed = mixed / jnp.transpose(totals, (2, 0, 1))[..., None]
        return mixed.reshape(DRAFT, QW).astype(jnp.bfloat16)
    attention = lax.map(attend, (queries.reshape(REQUESTS, DRAFT, QW), draft_entries[0].reshape(REQUESTS, DRAFT, KW), draft_entries[1].reshape(REQUESTS, DRAFT, KW), page_index, cache_len, reached))
    attention = attention.reshape(TOKENS, QW)
    residual = (hidden.astype(jnp.float32) + jnp.dot(attention, out_proj, preferred_element_type=jnp.float32)).astype(jnp.bfloat16)
    residual_wide = residual.astype(jnp.float32)
    scale_rows = lax.rsqrt(lax.optimization_barrier(jnp.mean(residual_wide * residual_wide, axis=-1, keepdims=True)) + NORM_EPSILON)
    normed = (residual_wide * scale_rows * norm_gain.astype(jnp.float32)).astype(jnp.bfloat16)
    block_count = TOKENS // TOK_DEV
    block_rows = TOK_DEV * TOP
    flat_experts = expert_ids.reshape(block_count, block_rows)
    expert_range = jnp.arange(EXPERTS, dtype=jnp.int32)
    onehot = (flat_experts[:, :, None] == expert_range[None, None, :]).astype(jnp.int32)
    slot_index = lax.optimization_barrier(jnp.sum((jnp.cumsum(onehot, axis=1) - 1) * onehot, axis=2))
    block_index = jnp.arange(block_count, dtype=jnp.int32)[:, None]
    destinations = flat_experts * (block_count * CAP) + block_index * CAP + slot_index
    token_index = block_index * TOK_DEV + jnp.arange(block_rows, dtype=jnp.int32)[None, :] // TOP
    slot_count = EXPERTS * block_count * CAP
    source_rows = jnp.full((slot_count,), TOKENS, jnp.int32).at[destinations.reshape(-1)].set(token_index.reshape(-1))
    slot_weights = jnp.zeros((slot_count,), jnp.float32).at[destinations.reshape(-1)].set(expert_weights.reshape(-1))
    source_rows = source_rows.reshape(EXPERTS, block_count * CAP)
    slot_weights = slot_weights.reshape(EXPERTS, block_count * CAP)
    padded = jnp.concatenate([normed, jnp.zeros((1, D), jnp.bfloat16)], axis=0)

    def one_expert(running, items):
        row_index, row_weights, gate_rows, upper_rows, down_rows = items
        inputs = padded[row_index].astype(jnp.float32)
        gate_values = jnp.einsum('rd,fd->rf', inputs, gate_rows.astype(jnp.float32))
        upper_values = jnp.einsum('rd,fd->rf', inputs, upper_rows.astype(jnp.float32))
        inner = lax.optimization_barrier((jax.nn.silu(gate_values) * upper_values).astype(jnp.bfloat16)).astype(jnp.float32)
        part_terms = jnp.einsum('rqf,qfd->rqd', inner.reshape(-1, DP_SPAN, FF_PART), down_rows.astype(jnp.float32).reshape(DP_SPAN, FF_PART, D))
        part_terms = lax.optimization_barrier(part_terms.astype(jnp.bfloat16)).astype(jnp.float32)
        expert_out = lax.optimization_barrier(lax.optimization_barrier(jnp.sum(part_terms, axis=1)).astype(jnp.bfloat16)).astype(jnp.float32)
        return (running.at[row_index].add(expert_out * row_weights[:, None], mode='drop'), None)
    routed, unused = lax.scan(one_expert, jnp.zeros((TOKENS, D), jnp.float32), (source_rows, slot_weights, expert_gate, expert_up, expert_down))
    shared_sum = jnp.zeros((TOKENS, D), jnp.float32)
    for section in range(DP_SPAN):
        first_unit = section * SH_PART
        gate_values = jnp.dot(normed, shared_gate[first_unit:first_unit + SH_PART].T, preferred_element_type=jnp.float32)
        upper_values = jnp.dot(normed, shared_up[first_unit:first_unit + SH_PART].T, preferred_element_type=jnp.float32)
        shared_inner = (jax.nn.silu(gate_values) * upper_values).astype(jnp.bfloat16)
        shared_term = jnp.dot(shared_inner, shared_down[first_unit:first_unit + SH_PART], preferred_element_type=jnp.float32).astype(jnp.bfloat16)
        shared_sum = shared_sum + shared_term.astype(jnp.float32)
    return (residual.astype(jnp.float32) + routed + shared_sum).astype(jnp.bfloat16)
```

```python
import jax
import jax.numpy as jnp
from jax import lax
from jax.sharding import PartitionSpec as P

HEADS = 16
KVH = 4
HD = 128
CAP = 16


NEG_FILL = -1e30
NORM_EPSILON = 1e-06
HIGHEST_PRECISION = lax.Precision.HIGHEST


def tree_reach(parents):
    node_count = parents.shape[-1]
    node_index = jnp.arange(node_count, dtype=jnp.int32)
    linked = (parents[:, :, None] == node_index[None, None, :]).astype(jnp.float32)
    reached = jnp.minimum(linked + jnp.eye(node_count, dtype=jnp.float32)[None], 1.0)
    for rounds in range(max(1, (node_count - 1).bit_length())):
        reached = jnp.minimum(
            jnp.einsum("rij,rjk->rik", reached, reached, precision=HIGHEST_PRECISION), 1.0
        )
    return reached


def score_block(query_heads, key_rows, live_mask):
    raw_scores = jnp.einsum(
        "rtgnd,rcgd->rgntc", query_heads, key_rows, preferred_element_type=jnp.float32
    ) * key_rows.shape[-1] ** (-0.5)
    wide_mask = live_mask[:, None, None]
    return (jnp.where(wide_mask, raw_scores, NEG_FILL), wide_mask)


def fold_keys(carry_state, scores, wide_mask, value_rows):
    running_top, running_total, running_sum = carry_state
    fresh_top = jnp.maximum(running_top, jnp.max(scores, axis=-1))
    rescale = jnp.exp(running_top - fresh_top)
    exponents = jnp.where(wide_mask, jnp.exp(scores - fresh_top[..., None]), 0.0)
    weights = exponents.astype(jnp.bfloat16)
    new_total = running_total * rescale + jnp.sum(exponents, axis=-1)
    mixed = jnp.einsum("rgntc,rcgd->rtgnd", weights, value_rows, preferred_element_type=jnp.float32)
    new_sum = running_sum * jnp.transpose(rescale, (0, 3, 1, 2))[..., None] + mixed
    return (fresh_top, new_total, new_sum)


def pool_state(carry_state, query_heads, table_rows, lengths, pieces):
    piece_keys, piece_values = pieces
    piece_count = piece_keys.shape[0]
    request_count, pages_per = table_rows.shape
    page_size = piece_keys.shape[1]
    key_heads = query_heads.shape[2]
    inside = (table_rows >= 0) & (table_rows < piece_count)
    picked = jnp.clip(table_rows, 0, piece_count - 1)
    cache_keys = piece_keys[picked].reshape(request_count, pages_per * page_size, key_heads, -1)
    cache_values = piece_values[picked].reshape(request_count, pages_per * page_size, key_heads, -1)
    positions = jnp.arange(pages_per * page_size, dtype=jnp.int32)
    usable = jnp.repeat(inside, page_size, axis=1) & (positions[None, :] < lengths[:, None])
    live_mask = jnp.broadcast_to(
        usable[:, None, :], (request_count, query_heads.shape[1], pages_per * page_size)
    )
    scores, wide_mask = score_block(query_heads, cache_keys, live_mask)
    return fold_keys(carry_state, scores, wide_mask, cache_values)


def blank_state(request_count, draft_nodes, key_heads, group_size, head_size):
    return (
        jnp.full((request_count, key_heads, group_size, draft_nodes), NEG_FILL, jnp.float32),
        jnp.zeros((request_count, key_heads, group_size, draft_nodes), jnp.float32),
        jnp.zeros((request_count, draft_nodes, key_heads, group_size, head_size), jnp.float32),
    )


def expert_block(grouped, gate_rows, upper_rows, down_rows):
    gate_values = jnp.einsum(
        "sekd,efd->sekf", grouped, gate_rows, preferred_element_type=jnp.float32
    )
    upper_values = jnp.einsum(
        "sekd,efd->sekf", grouped, upper_rows, preferred_element_type=jnp.float32
    )
    inner = (jax.nn.silu(gate_values) * upper_values).astype(jnp.bfloat16)
    return jnp.einsum("sekf,efd->sekd", inner, down_rows, preferred_element_type=jnp.float32)


def shared_block(tokens, gate_rows, upper_rows, down_rows):
    gate_values = jnp.einsum("td,fd->tf", tokens, gate_rows, preferred_element_type=jnp.float32)
    upper_values = jnp.einsum("td,fd->tf", tokens, upper_rows, preferred_element_type=jnp.float32)
    inner = (jax.nn.silu(gate_values) * upper_values).astype(jnp.bfloat16)
    return jnp.dot(inner, down_rows, preferred_element_type=jnp.float32)


def on_device(
    hidden,
    queries,
    draft_entries,
    key_pool,
    value_pool,
    page_table,
    cache_len,
    parents,
    out_proj,
    norm_gain,
    expert_gate,
    expert_up,
    expert_down,
    shared_gate,
    shared_up,
    shared_down,
    expert_ids,
    expert_weights,
):
    tok_rows, model_width = hidden.shape
    local_requests, draft_nodes = parents.shape
    group_size = HEADS // KVH
    query_heads = queries.reshape(local_requests, draft_nodes, KVH, group_size, HD)
    draft_keys = draft_entries[0].reshape(local_requests, draft_nodes, KVH, HD)
    draft_values = draft_entries[1].reshape(local_requests, draft_nodes, KVH, HD)
    reached = tree_reach(parents)
    tree_scores, tree_mask = score_block(query_heads, draft_keys, reached > 0.5)
    tree_state = fold_keys(
        blank_state(local_requests, draft_nodes, KVH, group_size, HD),
        tree_scores,
        tree_mask,
        draft_values,
    )
    both_pools = lax.all_gather(jnp.stack([key_pool, value_pool]), "dp", axis=1, tiled=True)
    final_top, final_total, final_sum = pool_state(
        tree_state,
        query_heads,
        page_table,
        cache_len,
        (both_pools[0], both_pools[1]),
    )
    attention = (
        (final_sum / jnp.transpose(final_total, (0, 3, 1, 2))[..., None])
        .reshape(tok_rows, queries.shape[1])
        .astype(jnp.bfloat16)
    )
    residual = (
        hidden.astype(jnp.float32)
        + jnp.dot(attention, out_proj, preferred_element_type=jnp.float32)
    ).astype(jnp.bfloat16)
    residual_wide = residual.astype(jnp.float32)
    scale_rows = lax.rsqrt(
        jnp.mean(residual_wide * residual_wide, axis=-1, keepdims=True) + NORM_EPSILON
    )
    normed = (residual_wide * scale_rows * norm_gain.astype(jnp.float32)).astype(jnp.bfloat16)
    local_experts = expert_gate.shape[0]
    column_count = lax.axis_size("exp")
    row_count = lax.axis_size("dp")
    expert_count = local_experts * column_count
    slot_total = expert_count * CAP
    flat_experts = expert_ids.reshape(-1)
    onehot = (flat_experts[:, None] == jnp.arange(expert_count, dtype=jnp.int32)[None, :]).astype(
        jnp.int32
    )
    slot_ids = jnp.sum((jnp.cumsum(onehot, axis=0) - 1) * onehot, axis=1)
    destinations = (flat_experts * CAP + slot_ids).reshape(expert_ids.shape)
    slot_hits = destinations[:, :, None] == jnp.arange(slot_total, dtype=jnp.int32)[None, None, :]
    placement = jnp.sum(slot_hits.astype(jnp.bfloat16), axis=1)
    outgoing = jnp.einsum(
        "ts,td->sd", placement, normed, preferred_element_type=jnp.float32
    ).astype(jnp.bfloat16)
    outgoing = outgoing.reshape(column_count, local_experts * CAP, model_width)
    arrived = lax.all_to_all(outgoing, "exp", split_axis=0, concat_axis=0, tiled=True)
    arrived = arrived.reshape(column_count * local_experts * CAP, model_width)
    gathered = lax.all_gather(
        jnp.concatenate([arrived, normed], axis=0), "dp", axis=0, tiled=False
    )
    arrived_rows = column_count * local_experts * CAP
    grouped = gathered[:, :arrived_rows].reshape(
        row_count * column_count, local_experts, CAP, model_width
    )
    group_tokens = gathered[:, arrived_rows:].reshape(row_count * tok_rows, model_width)
    routed_terms = expert_block(grouped, expert_gate, expert_up, expert_down)
    shared_terms = shared_block(group_tokens, shared_gate, shared_up, shared_down)
    both_terms = jnp.concatenate(
        [
            routed_terms.astype(jnp.bfloat16).reshape(row_count, arrived_rows, model_width),
            shared_terms.astype(jnp.bfloat16).reshape(row_count, tok_rows, model_width),
        ],
        axis=1,
    )
    both_sums = lax.psum_scatter(both_terms, "dp", scatter_dimension=0, tiled=False)
    routed_sum = both_sums[:arrived_rows]
    shared_sum = both_sums[arrived_rows:].astype(jnp.float32)
    returned = lax.all_to_all(
        routed_sum.reshape(column_count, local_experts * CAP, model_width),
        "exp",
        split_axis=0,
        concat_axis=0,
        tiled=True,
    )
    returned_rows = returned.reshape(slot_total, model_width)
    slot_weights = jnp.sum(
        jnp.where(slot_hits, expert_weights[:, :, None], 0.0), axis=1
    )
    weights_high = slot_weights.astype(jnp.bfloat16)
    weights_low = (slot_weights - weights_high.astype(jnp.float32)).astype(jnp.bfloat16)
    routed_out = jnp.dot(
        weights_high, returned_rows, preferred_element_type=jnp.float32
    ) + jnp.dot(weights_low, returned_rows, preferred_element_type=jnp.float32)
    return (residual.astype(jnp.float32) + routed_out + shared_sum).astype(jnp.bfloat16)


def solution(mesh):
    placed = (
        P(("dp", "exp"), None),
        P(("dp", "exp"), None),
        P(None, ("dp", "exp"), None),
        P(("dp", "exp"), None, None),
        P(("dp", "exp"), None, None),
        P(("dp", "exp"), None),
        P(("dp", "exp")),
        P(("dp", "exp"), None),
        P(),
        P(),
        P("exp", "dp", None),
        P("exp", "dp", None),
        P("exp", "dp", None),
        P("dp", None),
        P("dp", None),
        P("dp", None),
        P(("dp", "exp"), None),
        P(("dp", "exp"), None),
    )
    return jax.shard_map(
        on_device, mesh=mesh, in_specs=placed, out_specs=P(("dp", "exp"), None), check_vma=False
    )
```

```python
import jax
import jax.numpy as jnp
from jax import lax
from jax.sharding import PartitionSpec as P

HEADS = 16
KVH = 4
HD = 128
CAP = 16


NEG_FILL = -1e30
NORM_EPSILON = 1e-06
HIGHEST_PRECISION = lax.Precision.HIGHEST


def tree_reach(parents):
    node_count = parents.shape[-1]
    node_index = jnp.arange(node_count, dtype=jnp.int32)
    linked = (parents[:, :, None] == node_index[None, None, :]).astype(jnp.float32)
    reached = jnp.minimum(linked + jnp.eye(node_count, dtype=jnp.float32)[None], 1.0)
    for rounds in range(max(1, (node_count - 1).bit_length())):
        reached = jnp.minimum(
            jnp.einsum("rij,rjk->rik", reached, reached, precision=HIGHEST_PRECISION), 1.0
        )
    return reached


def score_block(query_heads, key_rows, live_mask):
    raw_scores = jnp.einsum(
        "rtgnd,rcgd->rgntc", query_heads, key_rows, preferred_element_type=jnp.float32
    ) * key_rows.shape[-1] ** (-0.5)
    wide_mask = live_mask[:, None, None]
    return (jnp.where(wide_mask, raw_scores, NEG_FILL), wide_mask)


def fold_keys(carry_state, scores, wide_mask, value_rows):
    running_top, running_total, running_sum = carry_state
    fresh_top = jnp.maximum(running_top, jnp.max(scores, axis=-1))
    rescale = jnp.exp(running_top - fresh_top)
    exponents = jnp.where(wide_mask, jnp.exp(scores - fresh_top[..., None]), 0.0)
    weights = exponents.astype(jnp.bfloat16)
    new_total = running_total * rescale + jnp.sum(exponents, axis=-1)
    mixed = jnp.einsum("rgntc,rcgd->rtgnd", weights, value_rows, preferred_element_type=jnp.float32)
    new_sum = running_sum * jnp.transpose(rescale, (0, 3, 1, 2))[..., None] + mixed
    return (fresh_top, new_total, new_sum)


def pool_state(carry_state, query_heads, table_rows, lengths, pieces):
    piece_count = pieces.shape[1]
    request_count, pages_per = table_rows.shape
    page_size = pieces.shape[2]
    key_heads = query_heads.shape[2]
    inside = (table_rows >= 0) & (table_rows < piece_count)
    picked = jnp.clip(table_rows, 0, piece_count - 1)
    picked_pages = pieces[:, picked]
    cache_keys = picked_pages[0].reshape(request_count, pages_per * page_size, key_heads, -1)
    cache_values = picked_pages[1].reshape(request_count, pages_per * page_size, key_heads, -1)
    positions = jnp.arange(pages_per * page_size, dtype=jnp.int32)
    usable = jnp.repeat(inside, page_size, axis=1) & (positions[None, :] < lengths[:, None])
    live_mask = jnp.broadcast_to(
        usable[:, None, :], (request_count, query_heads.shape[1], pages_per * page_size)
    )
    scores, wide_mask = score_block(query_heads, cache_keys, live_mask)
    return fold_keys(carry_state, scores, wide_mask, cache_values)


def blank_state(request_count, draft_nodes, key_heads, group_size, head_size):
    return (
        jnp.full((request_count, key_heads, group_size, draft_nodes), NEG_FILL, jnp.float32),
        jnp.zeros((request_count, key_heads, group_size, draft_nodes), jnp.float32),
        jnp.zeros((request_count, draft_nodes, key_heads, group_size, head_size), jnp.float32),
    )


def expert_block(grouped, gate_rows, upper_rows, down_rows):
    gate_values = jnp.einsum(
        "sekd,efd->sekf", grouped, gate_rows, preferred_element_type=jnp.float32
    )
    upper_values = jnp.einsum(
        "sekd,efd->sekf", grouped, upper_rows, preferred_element_type=jnp.float32
    )
    inner = (jax.nn.silu(gate_values) * upper_values).astype(jnp.bfloat16)
    return jnp.einsum("sekf,efd->sekd", inner, down_rows, preferred_element_type=jnp.float32)


def shared_block(tokens, gate_rows, upper_rows, down_rows):
    gate_values = jnp.einsum("td,fd->tf", tokens, gate_rows, preferred_element_type=jnp.float32)
    upper_values = jnp.einsum("td,fd->tf", tokens, upper_rows, preferred_element_type=jnp.float32)
    inner = (jax.nn.silu(gate_values) * upper_values).astype(jnp.bfloat16)
    return jnp.dot(inner, down_rows, preferred_element_type=jnp.float32)


def on_device(
    hidden,
    queries,
    draft_entries,
    key_pool,
    value_pool,
    page_table,
    cache_len,
    parents,
    out_proj,
    norm_gain,
    expert_gate,
    expert_up,
    expert_down,
    shared_gate,
    shared_up,
    shared_down,
    expert_ids,
    expert_weights,
):
    tok_rows, model_width = hidden.shape
    local_requests, draft_nodes = parents.shape
    group_size = HEADS // KVH
    query_heads = queries.reshape(local_requests, draft_nodes, KVH, group_size, HD)
    draft_keys = draft_entries[0].reshape(local_requests, draft_nodes, KVH, HD)
    draft_values = draft_entries[1].reshape(local_requests, draft_nodes, KVH, HD)
    reached = tree_reach(parents)
    tree_scores, tree_mask = score_block(query_heads, draft_keys, reached > 0.5)
    tree_state = fold_keys(
        blank_state(local_requests, draft_nodes, KVH, group_size, HD),
        tree_scores,
        tree_mask,
        draft_values,
    )
    both_pools = lax.all_gather(jnp.stack([key_pool, value_pool]), "dp", axis=1, tiled=True)
    group_picks = lax.all_gather(
        jnp.concatenate([expert_ids.astype(jnp.float32), expert_weights], axis=1),
        "dp",
        axis=0,
        tiled=True,
    )
    final_top, final_total, final_sum = pool_state(
        tree_state,
        query_heads,
        page_table,
        cache_len,
        both_pools,
    )
    attention = (
        (final_sum / jnp.transpose(final_total, (0, 3, 1, 2))[..., None])
        .reshape(tok_rows, queries.shape[1])
        .astype(jnp.bfloat16)
    )
    residual = (
        hidden.astype(jnp.float32)
        + jnp.dot(attention, out_proj, preferred_element_type=jnp.float32)
    ).astype(jnp.bfloat16)
    residual_wide = residual.astype(jnp.float32)
    scale_rows = lax.rsqrt(
        jnp.mean(residual_wide * residual_wide, axis=-1, keepdims=True) + NORM_EPSILON
    )
    normed = (residual_wide * scale_rows * norm_gain.astype(jnp.float32)).astype(jnp.bfloat16)
    column_count = lax.axis_size("exp")
    row_count = lax.axis_size("dp")
    pick_count = expert_ids.shape[1]
    near_cap = CAP
    far_cap = CAP * row_count
    group_tokens = lax.all_gather(normed, "dp", axis=0, tiled=True)
    group_ids = group_picks[:, :pick_count].astype(jnp.int32)
    group_weights = group_picks[:, pick_count:]

    def slot_plan(ids, weights, parity, cap):
        token_count = ids.shape[0]
        picks = ((ids // 2)[:, :, None] == jnp.arange(column_count, dtype=jnp.int32)[None, None, :]) & (
            (ids % 2) == parity
        )[:, :, None]
        member = jnp.any(picks, axis=1)
        token_weight = jnp.sum(jnp.where(picks, weights[:, :, None], 0.0), axis=1)
        earlier = (
            jnp.arange(token_count, dtype=jnp.int32)[:, None]
            > jnp.arange(token_count, dtype=jnp.int32)[None, :]
        ).astype(jnp.bfloat16)
        rank = jnp.dot(
            earlier, member.astype(jnp.bfloat16), preferred_element_type=jnp.float32
        ).astype(jnp.int32)
        place = member[:, :, None] & (
            rank[:, :, None] == jnp.arange(cap, dtype=jnp.int32)[None, None, :]
        )
        slot_weights = jnp.where(place, token_weight[:, :, None], 0.0)
        return (
            place.reshape(token_count, column_count * cap),
            slot_weights.reshape(token_count, column_count * cap),
        )

    near_place, near_weights = slot_plan(expert_ids, expert_weights, 0, near_cap)
    far_place, far_weights = slot_plan(group_ids, group_weights, 1, far_cap)
    near_out = jnp.einsum(
        "ts,td->sd",
        near_place.astype(jnp.bfloat16),
        normed,
        preferred_element_type=jnp.float32,
    ).astype(jnp.bfloat16)
    far_out = jnp.einsum(
        "ts,td->sd",
        far_place.astype(jnp.bfloat16),
        group_tokens,
        preferred_element_type=jnp.float32,
    ).astype(jnp.bfloat16)
    near_arrived = lax.all_to_all(
        near_out.reshape(column_count, near_cap, model_width),
        "exp",
        split_axis=0,
        concat_axis=0,
        tiled=True,
    )
    far_arrived = lax.all_to_all(
        far_out.reshape(column_count, far_cap, model_width),
        "exp",
        split_axis=0,
        concat_axis=0,
        tiled=True,
    )
    near_rows = lax.all_gather(near_arrived, "dp", axis=0, tiled=True).reshape(-1, model_width)
    far_rows = far_arrived.reshape(-1, model_width)
    near_terms = shared_block(near_rows, expert_gate[0], expert_up[0], expert_down[0])
    far_terms = shared_block(far_rows, expert_gate[1], expert_up[1], expert_down[1])
    shared_terms = shared_block(group_tokens, shared_gate, shared_up, shared_down)
    near_sum = lax.psum_scatter(
        near_terms.astype(jnp.bfloat16).reshape(row_count, column_count, near_cap, model_width),
        "dp",
        scatter_dimension=0,
        tiled=False,
    )
    far_back = lax.all_to_all(
        far_terms.astype(jnp.bfloat16).reshape(column_count, far_cap, model_width),
        "exp",
        split_axis=0,
        concat_axis=0,
        tiled=True,
    ).reshape(-1, model_width)
    near_back = lax.all_to_all(
        near_sum, "exp", split_axis=0, concat_axis=0, tiled=True
    ).reshape(-1, model_width)

    def combine(slot_weights, rows):
        return jnp.dot(slot_weights.astype(jnp.bfloat16), rows, preferred_element_type=jnp.float32)

    far_part = combine(far_weights, far_back) + shared_terms.astype(
        jnp.bfloat16
    ).astype(jnp.float32)
    far_sum = lax.psum_scatter(
        far_part.astype(jnp.bfloat16).reshape(row_count, tok_rows, model_width),
        "dp",
        scatter_dimension=0,
        tiled=False,
    ).astype(jnp.float32)
    near_part = combine(near_weights, near_back)
    return (residual.astype(jnp.float32) + near_part + far_sum).astype(jnp.bfloat16)


def solution(mesh):
    placed = (
        P(("dp", "exp"), None),
        P(("dp", "exp"), None),
        P(None, ("dp", "exp"), None),
        P(("dp", "exp"), None, None),
        P(("dp", "exp"), None, None),
        P(("dp", "exp"), None),
        P(("dp", "exp")),
        P(("dp", "exp"), None),
        P(),
        P(),
        P("exp", "dp", None),
        P("exp", "dp", None),
        P("exp", "dp", None),
        P("dp", None),
        P("dp", None),
        P("dp", None),
        P(("dp", "exp"), None),
        P(("dp", "exp"), None),
    )
    return jax.shard_map(
        on_device, mesh=mesh, in_specs=placed, out_specs=P(("dp", "exp"), None), check_vma=False
    )
```

```python
import jax
import jax.numpy as jnp
from jax import lax
from jax.sharding import PartitionSpec as P

HEADS = 16
KVH = 4
HD = 128
CAP = 16


NEG_FILL = -1e30
NORM_EPSILON = 1e-06
HIGHEST_PRECISION = lax.Precision.HIGHEST


def tree_reach(parents):
    node_count = parents.shape[-1]
    node_index = jnp.arange(node_count, dtype=jnp.int32)
    linked = (parents[:, :, None] == node_index[None, None, :]).astype(jnp.float32)
    reached = jnp.minimum(linked + jnp.eye(node_count, dtype=jnp.float32)[None], 1.0)
    for rounds in range(max(1, (node_count - 1).bit_length())):
        reached = jnp.minimum(
            jnp.einsum("rij,rjk->rik", reached, reached, precision=HIGHEST_PRECISION), 1.0
        )
    return reached


def score_block(query_heads, key_rows, live_mask):
    raw_scores = jnp.einsum(
        "rtgnd,rcgd->rgntc", query_heads, key_rows, preferred_element_type=jnp.float32
    ) * key_rows.shape[-1] ** (-0.5)
    wide_mask = live_mask[:, None, None]
    return (jnp.where(wide_mask, raw_scores, NEG_FILL), wide_mask)


def fold_keys(carry_state, scores, wide_mask, value_rows):
    running_top, running_total, running_sum = carry_state
    fresh_top = jnp.maximum(running_top, jnp.max(scores, axis=-1))
    rescale = jnp.exp(running_top - fresh_top)
    exponents = jnp.where(wide_mask, jnp.exp(scores - fresh_top[..., None]), 0.0)
    weights = exponents.astype(jnp.bfloat16)
    new_total = running_total * rescale + jnp.sum(exponents, axis=-1)
    mixed = jnp.einsum("rgntc,rcgd->rtgnd", weights, value_rows, preferred_element_type=jnp.float32)
    new_sum = running_sum * jnp.transpose(rescale, (0, 3, 1, 2))[..., None] + mixed
    return (fresh_top, new_total, new_sum)


def pool_state(carry_state, query_heads, table_rows, lengths, pieces):
    piece_count = pieces.shape[1]
    request_count, pages_per = table_rows.shape
    page_size = pieces.shape[2]
    key_heads = query_heads.shape[2]
    inside = (table_rows >= 0) & (table_rows < piece_count)
    picked = jnp.clip(table_rows, 0, piece_count - 1)
    picked_pages = pieces[:, picked]
    cache_keys = picked_pages[0].reshape(request_count, pages_per * page_size, key_heads, -1)
    cache_values = picked_pages[1].reshape(request_count, pages_per * page_size, key_heads, -1)
    positions = jnp.arange(pages_per * page_size, dtype=jnp.int32)
    usable = jnp.repeat(inside, page_size, axis=1) & (positions[None, :] < lengths[:, None])
    live_mask = jnp.broadcast_to(
        usable[:, None, :], (request_count, query_heads.shape[1], pages_per * page_size)
    )
    scores, wide_mask = score_block(query_heads, cache_keys, live_mask)
    return fold_keys(carry_state, scores, wide_mask, cache_values)


def blank_state(request_count, draft_nodes, key_heads, group_size, head_size):
    return (
        jnp.full((request_count, key_heads, group_size, draft_nodes), NEG_FILL, jnp.float32),
        jnp.zeros((request_count, key_heads, group_size, draft_nodes), jnp.float32),
        jnp.zeros((request_count, draft_nodes, key_heads, group_size, head_size), jnp.float32),
    )


def expert_block(grouped, gate_rows, upper_rows, down_rows):
    gate_values = jnp.einsum(
        "sekd,efd->sekf", grouped, gate_rows, preferred_element_type=jnp.float32
    )
    upper_values = jnp.einsum(
        "sekd,efd->sekf", grouped, upper_rows, preferred_element_type=jnp.float32
    )
    inner = (jax.nn.silu(gate_values) * upper_values).astype(jnp.bfloat16)
    return jnp.einsum("sekf,efd->sekd", inner, down_rows, preferred_element_type=jnp.float32)


def shared_block(tokens, gate_rows, upper_rows, down_rows):
    gate_values = jnp.einsum("td,fd->tf", tokens, gate_rows, preferred_element_type=jnp.float32)
    upper_values = jnp.einsum("td,fd->tf", tokens, upper_rows, preferred_element_type=jnp.float32)
    inner = (jax.nn.silu(gate_values) * upper_values).astype(jnp.bfloat16)
    return jnp.dot(inner, down_rows, preferred_element_type=jnp.float32)


def on_device(
    hidden,
    queries,
    draft_entries,
    key_pool,
    value_pool,
    page_table,
    cache_len,
    parents,
    out_proj,
    norm_gain,
    expert_gate,
    expert_up,
    expert_down,
    shared_gate,
    shared_up,
    shared_down,
    expert_ids,
    expert_weights,
):
    tok_rows, model_width = hidden.shape
    group_picks = lax.all_gather(
        jnp.concatenate([expert_ids.astype(jnp.float32), expert_weights], axis=1),
        "dp",
        axis=0,
        tiled=True,
    )
    group_picks, queries, draft_entries = lax.optimization_barrier(
        (group_picks, queries, draft_entries)
    )
    local_requests, draft_nodes = parents.shape
    group_size = HEADS // KVH
    query_heads = queries.reshape(local_requests, draft_nodes, KVH, group_size, HD)
    draft_keys = draft_entries[0].reshape(local_requests, draft_nodes, KVH, HD)
    draft_values = draft_entries[1].reshape(local_requests, draft_nodes, KVH, HD)
    reached = tree_reach(parents)
    tree_scores, tree_mask = score_block(query_heads, draft_keys, reached > 0.5)
    tree_state = fold_keys(
        blank_state(local_requests, draft_nodes, KVH, group_size, HD),
        tree_scores,
        tree_mask,
        draft_values,
    )
    both_pools = lax.all_gather(jnp.stack([key_pool, value_pool]), "dp", axis=1, tiled=True)
    final_top, final_total, final_sum = pool_state(
        tree_state,
        query_heads,
        page_table,
        cache_len,
        both_pools,
    )
    attention = (
        (final_sum / jnp.transpose(final_total, (0, 3, 1, 2))[..., None])
        .reshape(tok_rows, queries.shape[1])
        .astype(jnp.bfloat16)
    )
    residual = (
        hidden.astype(jnp.float32)
        + jnp.dot(attention, out_proj, preferred_element_type=jnp.float32)
    ).astype(jnp.bfloat16)
    residual_wide = residual.astype(jnp.float32)
    scale_rows = lax.rsqrt(
        jnp.mean(residual_wide * residual_wide, axis=-1, keepdims=True) + NORM_EPSILON
    )
    normed = (residual_wide * scale_rows * norm_gain.astype(jnp.float32)).astype(jnp.bfloat16)
    column_count = lax.axis_size("exp")
    row_count = lax.axis_size("dp")
    pick_count = expert_ids.shape[1]
    near_cap = CAP
    far_cap = CAP * row_count
    group_tokens = lax.all_gather(normed, "dp", axis=0, tiled=True)
    group_ids = group_picks[:, :pick_count].astype(jnp.int32)
    group_weights = group_picks[:, pick_count:]

    def slot_plan(ids, weights, parity, cap):
        token_count = ids.shape[0]
        picks = ((ids // 2)[:, :, None] == jnp.arange(column_count, dtype=jnp.int32)[None, None, :]) & (
            (ids % 2) == parity
        )[:, :, None]
        member = jnp.any(picks, axis=1)
        token_weight = jnp.sum(jnp.where(picks, weights[:, :, None], 0.0), axis=1)
        earlier = (
            jnp.arange(token_count, dtype=jnp.int32)[:, None]
            > jnp.arange(token_count, dtype=jnp.int32)[None, :]
        ).astype(jnp.bfloat16)
        rank = jnp.dot(
            earlier, member.astype(jnp.bfloat16), preferred_element_type=jnp.float32
        ).astype(jnp.int32)
        place = member[:, :, None] & (
            rank[:, :, None] == jnp.arange(cap, dtype=jnp.int32)[None, None, :]
        )
        slot_weights = jnp.where(place, token_weight[:, :, None], 0.0)
        return (
            place.reshape(token_count, column_count * cap),
            slot_weights.reshape(token_count, column_count * cap),
        )

    near_place, near_weights = slot_plan(expert_ids, expert_weights, 0, near_cap)
    far_place, far_weights = slot_plan(group_ids, group_weights, 1, far_cap)
    near_out = jnp.einsum(
        "ts,td->sd",
        near_place.astype(jnp.bfloat16),
        normed,
        preferred_element_type=jnp.float32,
    ).astype(jnp.bfloat16)
    far_out = jnp.einsum(
        "ts,td->sd",
        far_place.astype(jnp.bfloat16),
        group_tokens,
        preferred_element_type=jnp.float32,
    ).astype(jnp.bfloat16)
    near_arrived = lax.all_to_all(
        near_out.reshape(column_count, near_cap, model_width),
        "exp",
        split_axis=0,
        concat_axis=0,
        tiled=True,
    )
    far_arrived = lax.all_to_all(
        far_out.reshape(column_count, far_cap, model_width),
        "exp",
        split_axis=0,
        concat_axis=0,
        tiled=True,
    )
    near_rows = lax.all_gather(near_arrived, "dp", axis=0, tiled=True).reshape(-1, model_width)
    far_rows = far_arrived.reshape(-1, model_width)
    near_terms = shared_block(near_rows, expert_gate[0], expert_up[0], expert_down[0])
    far_terms = shared_block(far_rows, expert_gate[1], expert_up[1], expert_down[1])
    shared_terms = shared_block(group_tokens, shared_gate, shared_up, shared_down)
    near_sum = lax.psum_scatter(
        near_terms.astype(jnp.bfloat16).reshape(row_count, column_count, near_cap, model_width),
        "dp",
        scatter_dimension=0,
        tiled=False,
    )
    far_back = lax.all_to_all(
        far_terms.astype(jnp.bfloat16).reshape(column_count, far_cap, model_width),
        "exp",
        split_axis=0,
        concat_axis=0,
        tiled=True,
    ).reshape(-1, model_width)
    near_back = lax.all_to_all(
        near_sum, "exp", split_axis=0, concat_axis=0, tiled=True
    ).reshape(-1, model_width)

    def combine(slot_weights, rows):
        return jnp.dot(slot_weights.astype(jnp.bfloat16), rows, preferred_element_type=jnp.float32)

    far_part = combine(far_weights, far_back) + shared_terms.astype(
        jnp.bfloat16
    ).astype(jnp.float32)
    far_sum = lax.psum_scatter(
        far_part.astype(jnp.bfloat16).reshape(row_count, tok_rows, model_width),
        "dp",
        scatter_dimension=0,
        tiled=False,
    ).astype(jnp.float32)
    near_part = combine(near_weights, near_back)
    return (residual.astype(jnp.float32) + near_part + far_sum).astype(jnp.bfloat16)


def solution(mesh):
    placed = (
        P(("dp", "exp"), None),
        P(("dp", "exp"), None),
        P(None, ("dp", "exp"), None),
        P(("dp", "exp"), None, None),
        P(("dp", "exp"), None, None),
        P(("dp", "exp"), None),
        P(("dp", "exp")),
        P(("dp", "exp"), None),
        P(),
        P(),
        P("exp", "dp", None),
        P("exp", "dp", None),
        P("exp", "dp", None),
        P("dp", None),
        P("dp", None),
        P("dp", None),
        P(("dp", "exp"), None),
        P(("dp", "exp"), None),
    )
    return jax.shard_map(
        on_device, mesh=mesh, in_specs=placed, out_specs=P(("dp", "exp"), None), check_vma=False
    )
```

```python
import jax
import jax.numpy as jnp
from jax import lax
from jax.sharding import PartitionSpec as P

HEADS = 16
KVH = 4
HD = 128
CAP = 16


NEG_FILL = -1e30
NORM_EPSILON = 1e-06
HIGHEST_PRECISION = lax.Precision.HIGHEST


def tree_reach(parents):
    node_count = parents.shape[-1]
    node_index = jnp.arange(node_count, dtype=jnp.int32)
    linked = (parents[:, :, None] == node_index[None, None, :]).astype(jnp.float32)
    reached = jnp.minimum(linked + jnp.eye(node_count, dtype=jnp.float32)[None], 1.0)
    for rounds in range(max(1, (node_count - 1).bit_length())):
        reached = jnp.minimum(
            jnp.einsum("rij,rjk->rik", reached, reached, precision=HIGHEST_PRECISION), 1.0
        )
    return reached


def score_block(query_heads, key_rows, live_mask):
    raw_scores = jnp.einsum(
        "rtgnd,rcgd->rgntc", query_heads, key_rows, preferred_element_type=jnp.float32
    ) * key_rows.shape[-1] ** (-0.5)
    wide_mask = live_mask[:, None, None]
    return (jnp.where(wide_mask, raw_scores, NEG_FILL), wide_mask)


def fold_keys(carry_state, scores, wide_mask, value_rows):
    running_top, running_total, running_sum = carry_state
    fresh_top = jnp.maximum(running_top, jnp.max(scores, axis=-1))
    rescale = jnp.exp(running_top - fresh_top)
    exponents = jnp.where(wide_mask, jnp.exp(scores - fresh_top[..., None]), 0.0)
    weights = exponents.astype(jnp.bfloat16)
    new_total = running_total * rescale + jnp.sum(exponents, axis=-1)
    mixed = jnp.einsum("rgntc,rcgd->rtgnd", weights, value_rows, preferred_element_type=jnp.float32)
    new_sum = running_sum * jnp.transpose(rescale, (0, 3, 1, 2))[..., None] + mixed
    return (fresh_top, new_total, new_sum)


def pool_state(carry_state, query_heads, table_rows, lengths, pieces):
    piece_count = pieces.shape[1]
    request_count, pages_per = table_rows.shape
    page_size = pieces.shape[2]
    key_heads = query_heads.shape[2]
    inside = (table_rows >= 0) & (table_rows < piece_count)
    picked = jnp.clip(table_rows, 0, piece_count - 1)
    picked_pages = pieces[:, picked]
    cache_keys = picked_pages[0].reshape(request_count, pages_per * page_size, key_heads, -1)
    cache_values = picked_pages[1].reshape(request_count, pages_per * page_size, key_heads, -1)
    positions = jnp.arange(pages_per * page_size, dtype=jnp.int32)
    usable = jnp.repeat(inside, page_size, axis=1) & (positions[None, :] < lengths[:, None])
    live_mask = jnp.broadcast_to(
        usable[:, None, :], (request_count, query_heads.shape[1], pages_per * page_size)
    )
    scores, wide_mask = score_block(query_heads, cache_keys, live_mask)
    return fold_keys(carry_state, scores, wide_mask, cache_values)


def blank_state(request_count, draft_nodes, key_heads, group_size, head_size):
    return (
        jnp.full((request_count, key_heads, group_size, draft_nodes), NEG_FILL, jnp.float32),
        jnp.zeros((request_count, key_heads, group_size, draft_nodes), jnp.float32),
        jnp.zeros((request_count, draft_nodes, key_heads, group_size, head_size), jnp.float32),
    )


def expert_block(grouped, gate_rows, upper_rows, down_rows):
    gate_values = jnp.einsum(
        "sekd,efd->sekf", grouped, gate_rows, preferred_element_type=jnp.float32
    )
    upper_values = jnp.einsum(
        "sekd,efd->sekf", grouped, upper_rows, preferred_element_type=jnp.float32
    )
    inner = (jax.nn.silu(gate_values) * upper_values).astype(jnp.bfloat16)
    return jnp.einsum("sekf,efd->sekd", inner, down_rows, preferred_element_type=jnp.float32)


def shared_block(tokens, gate_rows, upper_rows, down_rows):
    gate_values = jnp.einsum("td,fd->tf", tokens, gate_rows, preferred_element_type=jnp.float32)
    upper_values = jnp.einsum("td,fd->tf", tokens, upper_rows, preferred_element_type=jnp.float32)
    inner = (jax.nn.silu(gate_values) * upper_values).astype(jnp.bfloat16)
    return jnp.dot(inner, down_rows, preferred_element_type=jnp.float32)


def on_device(
    hidden,
    queries,
    draft_entries,
    key_pool,
    value_pool,
    page_table,
    cache_len,
    parents,
    out_proj,
    norm_gain,
    expert_gate,
    expert_up,
    expert_down,
    shared_gate,
    shared_up,
    shared_down,
    expert_ids,
    expert_weights,
):
    tok_rows, model_width = hidden.shape
    group_picks = lax.all_gather(
        jnp.concatenate([expert_ids.astype(jnp.float32), expert_weights], axis=1),
        "dp",
        axis=0,
        tiled=True,
    )
    group_picks, queries, draft_entries = lax.optimization_barrier(
        (group_picks, queries, draft_entries)
    )
    local_requests, draft_nodes = parents.shape
    group_size = HEADS // KVH
    query_heads = queries.reshape(local_requests, draft_nodes, KVH, group_size, HD)
    draft_keys = draft_entries[0].reshape(local_requests, draft_nodes, KVH, HD)
    draft_values = draft_entries[1].reshape(local_requests, draft_nodes, KVH, HD)
    reached = tree_reach(parents)
    tree_scores, tree_mask = score_block(query_heads, draft_keys, reached > 0.5)
    tree_state = fold_keys(
        blank_state(local_requests, draft_nodes, KVH, group_size, HD),
        tree_scores,
        tree_mask,
        draft_values,
    )
    own_pools = jnp.stack([key_pool, value_pool])
    row_span = lax.axis_size("dp")
    both_pools = jnp.concatenate(
        [own_pools]
        + [
            lax.ppermute(
                own_pools, "dp", [(i, (i + shift) % row_span) for i in range(row_span)]
            )
            for shift in range(1, row_span)
        ],
        axis=1,
    )
    pool_pages = key_pool.shape[0]
    page_table = (
        (lax.axis_index("dp") - page_table // pool_pages) % row_span * pool_pages
        + page_table % pool_pages
    )
    final_top, final_total, final_sum = pool_state(
        tree_state,
        query_heads,
        page_table,
        cache_len,
        both_pools,
    )
    attention = (
        (final_sum / jnp.transpose(final_total, (0, 3, 1, 2))[..., None])
        .reshape(tok_rows, queries.shape[1])
        .astype(jnp.bfloat16)
    )
    residual = (
        hidden.astype(jnp.float32)
        + jnp.dot(attention, out_proj, preferred_element_type=jnp.float32)
    ).astype(jnp.bfloat16)
    residual_wide = residual.astype(jnp.float32)
    scale_rows = lax.rsqrt(
        jnp.mean(residual_wide * residual_wide, axis=-1, keepdims=True) + NORM_EPSILON
    )
    normed = (residual_wide * scale_rows * norm_gain.astype(jnp.float32)).astype(jnp.bfloat16)
    column_count = lax.axis_size("exp")
    row_count = lax.axis_size("dp")
    pick_count = expert_ids.shape[1]
    near_cap = CAP
    far_cap = CAP * row_count
    group_tokens = lax.all_gather(normed, "dp", axis=0, tiled=True)
    group_ids = group_picks[:, :pick_count].astype(jnp.int32)
    group_weights = group_picks[:, pick_count:]

    def slot_plan(ids, weights, parity, cap):
        token_count = ids.shape[0]
        picks = ((ids // 2)[:, :, None] == jnp.arange(column_count, dtype=jnp.int32)[None, None, :]) & (
            (ids % 2) == parity
        )[:, :, None]
        member = jnp.any(picks, axis=1)
        token_weight = jnp.sum(jnp.where(picks, weights[:, :, None], 0.0), axis=1)
        earlier = (
            jnp.arange(token_count, dtype=jnp.int32)[:, None]
            > jnp.arange(token_count, dtype=jnp.int32)[None, :]
        ).astype(jnp.bfloat16)
        rank = jnp.dot(
            earlier, member.astype(jnp.bfloat16), preferred_element_type=jnp.float32
        ).astype(jnp.int32)
        place = member[:, :, None] & (
            rank[:, :, None] == jnp.arange(cap, dtype=jnp.int32)[None, None, :]
        )
        slot_weights = jnp.where(place, token_weight[:, :, None], 0.0)
        return (
            place.reshape(token_count, column_count * cap),
            slot_weights.reshape(token_count, column_count * cap),
        )

    near_place, near_weights = slot_plan(expert_ids, expert_weights, 0, near_cap)
    far_place, far_weights = slot_plan(group_ids, group_weights, 1, far_cap)
    near_out = jnp.einsum(
        "ts,td->sd",
        near_place.astype(jnp.bfloat16),
        normed,
        preferred_element_type=jnp.float32,
    ).astype(jnp.bfloat16)
    far_out = jnp.einsum(
        "ts,td->sd",
        far_place.astype(jnp.bfloat16),
        group_tokens,
        preferred_element_type=jnp.float32,
    ).astype(jnp.bfloat16)
    near_arrived = lax.all_to_all(
        near_out.reshape(column_count, near_cap, model_width),
        "exp",
        split_axis=0,
        concat_axis=0,
        tiled=True,
    )
    far_arrived = lax.all_to_all(
        far_out.reshape(column_count, far_cap, model_width),
        "exp",
        split_axis=0,
        concat_axis=0,
        tiled=True,
    )
    near_rows = lax.all_gather(near_arrived, "dp", axis=0, tiled=True).reshape(-1, model_width)
    far_rows = far_arrived.reshape(-1, model_width)
    near_terms = shared_block(near_rows, expert_gate[0], expert_up[0], expert_down[0])
    far_terms = shared_block(far_rows, expert_gate[1], expert_up[1], expert_down[1])
    shared_terms = shared_block(group_tokens, shared_gate, shared_up, shared_down)
    near_sum = lax.psum_scatter(
        near_terms.astype(jnp.bfloat16).reshape(row_count, column_count, near_cap, model_width),
        "dp",
        scatter_dimension=0,
        tiled=False,
    )
    far_back = lax.all_to_all(
        far_terms.astype(jnp.bfloat16).reshape(column_count, far_cap, model_width),
        "exp",
        split_axis=0,
        concat_axis=0,
        tiled=True,
    ).reshape(-1, model_width)
    near_back = lax.all_to_all(
        near_sum, "exp", split_axis=0, concat_axis=0, tiled=True
    ).reshape(-1, model_width)

    def combine(slot_weights, rows):
        return jnp.dot(slot_weights.astype(jnp.bfloat16), rows, preferred_element_type=jnp.float32)

    far_part = combine(far_weights, far_back) + shared_terms.astype(
        jnp.bfloat16
    ).astype(jnp.float32)
    far_sum = lax.psum_scatter(
        far_part.astype(jnp.bfloat16).reshape(row_count, tok_rows, model_width),
        "dp",
        scatter_dimension=0,
        tiled=False,
    ).astype(jnp.float32)
    near_part = combine(near_weights, near_back)
    return (residual.astype(jnp.float32) + near_part + far_sum).astype(jnp.bfloat16)


def solution(mesh):
    placed = (
        P(("dp", "exp"), None),
        P(("dp", "exp"), None),
        P(None, ("dp", "exp"), None),
        P(("dp", "exp"), None, None),
        P(("dp", "exp"), None, None),
        P(("dp", "exp"), None),
        P(("dp", "exp")),
        P(("dp", "exp"), None),
        P(),
        P(),
        P("exp", "dp", None),
        P("exp", "dp", None),
        P("exp", "dp", None),
        P("dp", None),
        P("dp", None),
        P("dp", None),
        P(("dp", "exp"), None),
        P(("dp", "exp"), None),
    )
    return jax.shard_map(
        on_device, mesh=mesh, in_specs=placed, out_specs=P(("dp", "exp"), None), check_vma=False
    )
```

```python
import jax
import jax.numpy as jnp
from jax import lax
from jax.sharding import PartitionSpec as P

HEADS = 16
KVH = 4
HD = 128
CAP = 16


NEG_FILL = -1e30
NORM_EPSILON = 1e-06
HIGHEST_PRECISION = lax.Precision.HIGHEST


def tree_reach(parents):
    node_count = parents.shape[-1]
    node_index = jnp.arange(node_count, dtype=jnp.int32)
    linked = (parents[:, :, None] == node_index[None, None, :]).astype(jnp.float32)
    reached = jnp.minimum(linked + jnp.eye(node_count, dtype=jnp.float32)[None], 1.0)
    for rounds in range(max(1, (node_count - 1).bit_length())):
        reached = jnp.minimum(
            jnp.einsum("rij,rjk->rik", reached, reached, precision=HIGHEST_PRECISION), 1.0
        )
    return reached


def score_block(query_heads, key_rows, live_mask):
    raw_scores = jnp.einsum(
        "rtgnd,rcgd->rgntc", query_heads, key_rows, preferred_element_type=jnp.float32
    ) * key_rows.shape[-1] ** (-0.5)
    wide_mask = live_mask[:, None, None]
    return (jnp.where(wide_mask, raw_scores, NEG_FILL), wide_mask)


def fold_keys(carry_state, scores, wide_mask, value_rows):
    running_top, running_total, running_sum = carry_state
    fresh_top = jnp.maximum(running_top, jnp.max(scores, axis=-1))
    rescale = jnp.exp(running_top - fresh_top)
    exponents = jnp.where(wide_mask, jnp.exp(scores - fresh_top[..., None]), 0.0)
    weights = exponents.astype(jnp.bfloat16)
    new_total = running_total * rescale + jnp.sum(exponents, axis=-1)
    mixed = jnp.einsum("rgntc,rcgd->rtgnd", weights, value_rows, preferred_element_type=jnp.float32)
    new_sum = running_sum * jnp.transpose(rescale, (0, 3, 1, 2))[..., None] + mixed
    return (fresh_top, new_total, new_sum)


def pool_state(carry_state, query_heads, table_rows, lengths, pieces):
    piece_count = pieces.shape[1]
    request_count, pages_per = table_rows.shape
    page_size = pieces.shape[2]
    key_heads = query_heads.shape[2]
    inside = (table_rows >= 0) & (table_rows < piece_count)
    picked = jnp.clip(table_rows, 0, piece_count - 1)
    picked_pages = pieces[:, picked]
    cache_keys = picked_pages[0].reshape(request_count, pages_per * page_size, key_heads, -1)
    cache_values = picked_pages[1].reshape(request_count, pages_per * page_size, key_heads, -1)
    positions = jnp.arange(pages_per * page_size, dtype=jnp.int32)
    usable = jnp.repeat(inside, page_size, axis=1) & (positions[None, :] < lengths[:, None])
    live_mask = jnp.broadcast_to(
        usable[:, None, :], (request_count, query_heads.shape[1], pages_per * page_size)
    )
    scores, wide_mask = score_block(query_heads, cache_keys, live_mask)
    return fold_keys(carry_state, scores, wide_mask, cache_values)


def blank_state(request_count, draft_nodes, key_heads, group_size, head_size):
    return (
        jnp.full((request_count, key_heads, group_size, draft_nodes), NEG_FILL, jnp.float32),
        jnp.zeros((request_count, key_heads, group_size, draft_nodes), jnp.float32),
        jnp.zeros((request_count, draft_nodes, key_heads, group_size, head_size), jnp.float32),
    )


def expert_block(grouped, gate_rows, upper_rows, down_rows):
    gate_values = jnp.einsum(
        "sekd,efd->sekf", grouped, gate_rows, preferred_element_type=jnp.float32
    )
    upper_values = jnp.einsum(
        "sekd,efd->sekf", grouped, upper_rows, preferred_element_type=jnp.float32
    )
    inner = (jax.nn.silu(gate_values) * upper_values).astype(jnp.bfloat16)
    return jnp.einsum("sekf,efd->sekd", inner, down_rows, preferred_element_type=jnp.float32)


def shared_block(tokens, gate_rows, upper_rows, down_rows):
    gate_values = jnp.einsum("td,fd->tf", tokens, gate_rows, preferred_element_type=jnp.float32)
    upper_values = jnp.einsum("td,fd->tf", tokens, upper_rows, preferred_element_type=jnp.float32)
    inner = (jax.nn.silu(gate_values) * upper_values).astype(jnp.bfloat16)
    return jnp.dot(inner, down_rows, preferred_element_type=jnp.float32)


def on_device(
    hidden,
    queries,
    draft_entries,
    key_pool,
    value_pool,
    page_table,
    cache_len,
    parents,
    out_proj,
    norm_gain,
    expert_gate,
    expert_up,
    expert_down,
    shared_gate,
    shared_up,
    shared_down,
    expert_ids,
    expert_weights,
):
    tok_rows, model_width = hidden.shape
    group_picks = lax.all_gather(
        jnp.concatenate([expert_ids.astype(jnp.float32), expert_weights], axis=1),
        "dp",
        axis=0,
        tiled=True,
    )
    group_picks, queries, draft_entries = lax.optimization_barrier(
        (group_picks, queries, draft_entries)
    )
    local_requests, draft_nodes = parents.shape
    group_size = HEADS // KVH
    query_heads = queries.reshape(local_requests, draft_nodes, KVH, group_size, HD)
    draft_keys = draft_entries[0].reshape(local_requests, draft_nodes, KVH, HD)
    draft_values = draft_entries[1].reshape(local_requests, draft_nodes, KVH, HD)
    reached = tree_reach(parents)
    tree_scores, tree_mask = score_block(query_heads, draft_keys, reached > 0.5)
    tree_state = fold_keys(
        blank_state(local_requests, draft_nodes, KVH, group_size, HD),
        tree_scores,
        tree_mask,
        draft_values,
    )
    both_pools = lax.all_gather(jnp.stack([key_pool, value_pool]), "dp", axis=1, tiled=True)
    final_top, final_total, final_sum = pool_state(
        tree_state,
        query_heads,
        page_table,
        cache_len,
        both_pools,
    )
    attention = (
        (final_sum / jnp.transpose(final_total, (0, 3, 1, 2))[..., None])
        .reshape(tok_rows, queries.shape[1])
        .astype(jnp.bfloat16)
    )
    residual = (
        hidden.astype(jnp.float32)
        + jnp.dot(attention, out_proj, preferred_element_type=jnp.float32)
    ).astype(jnp.bfloat16)
    residual_wide = residual.astype(jnp.float32)
    scale_rows = lax.rsqrt(
        jnp.mean(residual_wide * residual_wide, axis=-1, keepdims=True) + NORM_EPSILON
    )
    normed = (residual_wide * scale_rows * norm_gain.astype(jnp.float32)).astype(jnp.bfloat16)
    column_count = lax.axis_size("exp")
    row_count = lax.axis_size("dp")
    pick_count = expert_ids.shape[1]
    near_cap = CAP
    far_cap = CAP * row_count
    group_tokens = lax.all_gather(normed, "dp", axis=0, tiled=True)
    group_ids = group_picks[:, :pick_count].astype(jnp.int32)
    group_weights = group_picks[:, pick_count:]

    def slot_plan(ids, weights, parity, cap):
        token_count = ids.shape[0]
        picks = ((ids // 2)[:, :, None] == jnp.arange(column_count, dtype=jnp.int32)[None, None, :]) & (
            (ids % 2) == parity
        )[:, :, None]
        member = jnp.any(picks, axis=1)
        token_weight = jnp.sum(jnp.where(picks, weights[:, :, None], 0.0), axis=1)
        earlier = (
            jnp.arange(token_count, dtype=jnp.int32)[:, None]
            > jnp.arange(token_count, dtype=jnp.int32)[None, :]
        ).astype(jnp.bfloat16)
        rank = jnp.dot(
            earlier, member.astype(jnp.bfloat16), preferred_element_type=jnp.float32
        ).astype(jnp.int32)
        place = member[:, :, None] & (
            rank[:, :, None] == jnp.arange(cap, dtype=jnp.int32)[None, None, :]
        )
        slot_weights = jnp.where(place, token_weight[:, :, None], 0.0)
        return (
            place.reshape(token_count, column_count * cap),
            slot_weights.reshape(token_count, column_count * cap),
        )

    near_place, near_weights = slot_plan(expert_ids, expert_weights, 0, near_cap)
    far_place, far_weights = slot_plan(group_ids, group_weights, 1, far_cap)
    near_out = jnp.einsum(
        "ts,td->sd",
        near_place.astype(jnp.bfloat16),
        normed,
        preferred_element_type=jnp.float32,
    ).astype(jnp.bfloat16)
    far_out = jnp.einsum(
        "ts,td->sd",
        far_place.astype(jnp.bfloat16),
        group_tokens,
        preferred_element_type=jnp.float32,
    ).astype(jnp.bfloat16)
    near_arrived = lax.all_to_all(
        near_out.reshape(column_count, near_cap, model_width),
        "exp",
        split_axis=0,
        concat_axis=0,
        tiled=True,
    )
    far_arrived = lax.all_to_all(
        far_out.reshape(column_count, far_cap, model_width),
        "exp",
        split_axis=0,
        concat_axis=0,
        tiled=True,
    )
    near_rows = lax.all_gather(near_arrived, "dp", axis=0, tiled=True).reshape(-1, model_width)
    far_rows = far_arrived.reshape(-1, model_width)
    near_terms = shared_block(near_rows, expert_gate[0], expert_up[0], expert_down[0])
    far_terms = shared_block(far_rows, expert_gate[1], expert_up[1], expert_down[1])
    shared_terms = shared_block(group_tokens, shared_gate, shared_up, shared_down)
    near_sum = lax.psum_scatter(
        near_terms.astype(jnp.bfloat16).reshape(row_count, column_count, near_cap, model_width),
        "dp",
        scatter_dimension=0,
        tiled=False,
    )
    far_split = far_cap // 2
    far_quarter = far_split // row_count
    far_terms = far_terms.astype(jnp.bfloat16).reshape(column_count, far_cap, model_width)
    far_back = lax.all_to_all(
        far_terms[:, :far_split], "exp", split_axis=0, concat_axis=0, tiled=True
    ).reshape(-1, model_width)
    far_rest = lax.psum_scatter(
        jnp.transpose(
            far_terms[:, far_split:].reshape(column_count, row_count, far_quarter, model_width),
            (1, 0, 2, 3),
        ),
        "dp",
        scatter_dimension=0,
        tiled=False,
    )
    far_rest_back = lax.all_to_all(
        far_rest, "exp", split_axis=0, concat_axis=0, tiled=True
    ).reshape(-1, model_width)
    near_back = lax.all_to_all(
        near_sum, "exp", split_axis=0, concat_axis=0, tiled=True
    ).reshape(-1, model_width)

    def combine(slot_weights, rows):
        return jnp.dot(slot_weights.astype(jnp.bfloat16), rows, preferred_element_type=jnp.float32)

    far_grid = far_weights.reshape(-1, column_count, far_cap)
    rest_weights = lax.dynamic_slice_in_dim(
        far_grid, far_split + lax.axis_index("dp") * far_quarter, far_quarter, axis=2
    )
    far_part = (
        combine(far_grid[:, :, :far_split].reshape(-1, column_count * far_split), far_back)
        + combine(rest_weights.reshape(-1, column_count * far_quarter), far_rest_back)
        + shared_terms.astype(jnp.bfloat16).astype(jnp.float32)
    )
    far_sum = lax.psum_scatter(
        far_part.astype(jnp.bfloat16).reshape(row_count, tok_rows, model_width),
        "dp",
        scatter_dimension=0,
        tiled=False,
    ).astype(jnp.float32)
    near_part = combine(near_weights, near_back)
    return (residual.astype(jnp.float32) + near_part + far_sum).astype(jnp.bfloat16)


def solution(mesh):
    placed = (
        P(("dp", "exp"), None),
        P(("dp", "exp"), None),
        P(None, ("dp", "exp"), None),
        P(("dp", "exp"), None, None),
        P(("dp", "exp"), None, None),
        P(("dp", "exp"), None),
        P(("dp", "exp")),
        P(("dp", "exp"), None),
        P(),
        P(),
        P("exp", "dp", None),
        P("exp", "dp", None),
        P("exp", "dp", None),
        P("dp", None),
        P("dp", None),
        P("dp", None),
        P(("dp", "exp"), None),
        P(("dp", "exp"), None),
    )
    return jax.shard_map(
        on_device, mesh=mesh, in_specs=placed, out_specs=P(("dp", "exp"), None), check_vma=False
    )
```

```python
import jax
import jax.numpy as jnp
from jax import lax
from jax.sharding import PartitionSpec as P

HEADS = 16
KVH = 4
HD = 128
CAP = 16


NEG_FILL = -1e30
NORM_EPSILON = 1e-06
HIGHEST_PRECISION = lax.Precision.HIGHEST


def tree_reach(parents):
    node_count = parents.shape[-1]
    node_index = jnp.arange(node_count, dtype=jnp.int32)
    linked = (parents[:, :, None] == node_index[None, None, :]).astype(jnp.float32)
    reached = jnp.minimum(linked + jnp.eye(node_count, dtype=jnp.float32)[None], 1.0)
    for rounds in range(max(1, (node_count - 1).bit_length())):
        flags = reached.astype(jnp.bfloat16)
        reached = jnp.minimum(
            jnp.einsum("rij,rjk->rik", flags, flags, preferred_element_type=jnp.float32), 1.0
        )
    return reached


def score_block(query_heads, key_rows, live_mask):
    raw_scores = jnp.einsum(
        "rtgnd,rcgd->rgntc", query_heads, key_rows, preferred_element_type=jnp.float32
    ) * key_rows.shape[-1] ** (-0.5)
    wide_mask = live_mask[:, None, None]
    return (jnp.where(wide_mask, raw_scores, NEG_FILL), wide_mask)


def fold_keys(carry_state, scores, wide_mask, value_rows):
    running_top, running_total, running_sum = carry_state
    fresh_top = jnp.maximum(running_top, jnp.max(scores, axis=-1))
    rescale = jnp.exp(running_top - fresh_top)
    exponents = jnp.where(wide_mask, jnp.exp(scores - fresh_top[..., None]), 0.0)
    weights = exponents.astype(jnp.bfloat16)
    new_total = running_total * rescale + jnp.sum(exponents, axis=-1)
    mixed = jnp.einsum("rgntc,rcgd->rtgnd", weights, value_rows, preferred_element_type=jnp.float32)
    new_sum = running_sum * jnp.transpose(rescale, (0, 3, 1, 2))[..., None] + mixed
    return (fresh_top, new_total, new_sum)


def pool_state(carry_state, query_heads, table_rows, lengths, pieces):
    piece_count = pieces.shape[1]
    request_count, pages_per = table_rows.shape
    page_size = pieces.shape[2]
    key_heads = query_heads.shape[2]
    inside = (table_rows >= 0) & (table_rows < piece_count)
    picked = jnp.clip(table_rows, 0, piece_count - 1)
    picked_pages = pieces[:, picked]
    cache_keys = picked_pages[0].reshape(request_count, pages_per * page_size, key_heads, -1)
    cache_values = picked_pages[1].reshape(request_count, pages_per * page_size, key_heads, -1)
    positions = jnp.arange(pages_per * page_size, dtype=jnp.int32)
    usable = jnp.repeat(inside, page_size, axis=1) & (positions[None, :] < lengths[:, None])
    live_mask = jnp.broadcast_to(
        usable[:, None, :], (request_count, query_heads.shape[1], pages_per * page_size)
    )
    scores, wide_mask = score_block(query_heads, cache_keys, live_mask)
    return fold_keys(carry_state, scores, wide_mask, cache_values)


def blank_state(request_count, draft_nodes, key_heads, group_size, head_size):
    return (
        jnp.full((request_count, key_heads, group_size, draft_nodes), NEG_FILL, jnp.float32),
        jnp.zeros((request_count, key_heads, group_size, draft_nodes), jnp.float32),
        jnp.zeros((request_count, draft_nodes, key_heads, group_size, head_size), jnp.float32),
    )


def expert_block(grouped, gate_rows, upper_rows, down_rows):
    gate_values = jnp.einsum(
        "sekd,efd->sekf", grouped, gate_rows, preferred_element_type=jnp.float32
    )
    upper_values = jnp.einsum(
        "sekd,efd->sekf", grouped, upper_rows, preferred_element_type=jnp.float32
    )
    inner = (jax.nn.silu(gate_values) * upper_values).astype(jnp.bfloat16)
    return jnp.einsum("sekf,efd->sekd", inner, down_rows, preferred_element_type=jnp.float32)


def shared_block(tokens, gate_rows, upper_rows, down_rows):
    gate_values = jnp.einsum("td,fd->tf", tokens, gate_rows, preferred_element_type=jnp.float32)
    upper_values = jnp.einsum("td,fd->tf", tokens, upper_rows, preferred_element_type=jnp.float32)
    inner = (jax.nn.silu(gate_values) * upper_values).astype(jnp.bfloat16)
    return jnp.dot(inner, down_rows, preferred_element_type=jnp.float32)


def on_device(
    hidden,
    queries,
    draft_entries,
    key_pool,
    value_pool,
    page_table,
    cache_len,
    parents,
    out_proj,
    norm_gain,
    expert_gate,
    expert_up,
    expert_down,
    shared_gate,
    shared_up,
    shared_down,
    expert_ids,
    expert_weights,
):
    tok_rows, model_width = hidden.shape
    group_picks = lax.all_gather(
        jnp.concatenate([expert_ids.astype(jnp.float32), expert_weights], axis=1),
        "dp",
        axis=0,
        tiled=True,
    )
    group_picks, queries, draft_entries = lax.optimization_barrier(
        (group_picks, queries, draft_entries)
    )
    local_requests, draft_nodes = parents.shape
    group_size = HEADS // KVH
    query_heads = queries.reshape(local_requests, draft_nodes, KVH, group_size, HD)
    draft_keys = draft_entries[0].reshape(local_requests, draft_nodes, KVH, HD)
    draft_values = draft_entries[1].reshape(local_requests, draft_nodes, KVH, HD)
    reached = tree_reach(parents)
    tree_scores, tree_mask = score_block(query_heads, draft_keys, reached > 0.5)
    tree_state = fold_keys(
        blank_state(local_requests, draft_nodes, KVH, group_size, HD),
        tree_scores,
        tree_mask,
        draft_values,
    )
    both_pools = lax.all_gather(jnp.stack([key_pool, value_pool]), "dp", axis=1, tiled=True)
    final_top, final_total, final_sum = pool_state(
        tree_state,
        query_heads,
        page_table,
        cache_len,
        both_pools,
    )
    attention = (
        (final_sum / jnp.transpose(final_total, (0, 3, 1, 2))[..., None])
        .reshape(tok_rows, queries.shape[1])
        .astype(jnp.bfloat16)
    )
    residual = (
        hidden.astype(jnp.float32)
        + jnp.dot(attention, out_proj, preferred_element_type=jnp.float32)
    ).astype(jnp.bfloat16)
    residual_wide = residual.astype(jnp.float32)
    scale_rows = lax.rsqrt(
        jnp.mean(residual_wide * residual_wide, axis=-1, keepdims=True) + NORM_EPSILON
    )
    normed = (residual_wide * scale_rows * norm_gain.astype(jnp.float32)).astype(jnp.bfloat16)
    column_count = lax.axis_size("exp")
    row_count = lax.axis_size("dp")
    pick_count = expert_ids.shape[1]
    near_cap = CAP
    far_cap = CAP * row_count
    group_tokens = lax.all_gather(normed, "dp", axis=0, tiled=True)
    group_ids = group_picks[:, :pick_count].astype(jnp.int32)
    group_weights = group_picks[:, pick_count:]

    def slot_plan(ids, weights, parity, cap):
        token_count = ids.shape[0]
        picks = ((ids // 2)[:, :, None] == jnp.arange(column_count, dtype=jnp.int32)[None, None, :]) & (
            (ids % 2) == parity
        )[:, :, None]
        member = jnp.any(picks, axis=1)
        token_weight = jnp.sum(jnp.where(picks, weights[:, :, None], 0.0), axis=1)
        earlier = (
            jnp.arange(token_count, dtype=jnp.int32)[:, None]
            > jnp.arange(token_count, dtype=jnp.int32)[None, :]
        ).astype(jnp.bfloat16)
        rank = jnp.dot(
            earlier, member.astype(jnp.bfloat16), preferred_element_type=jnp.float32
        ).astype(jnp.int32)
        place = member[:, :, None] & (
            rank[:, :, None] == jnp.arange(cap, dtype=jnp.int32)[None, None, :]
        )
        slot_weights = jnp.where(place, token_weight[:, :, None], 0.0)
        return (
            place.reshape(token_count, column_count * cap),
            slot_weights.reshape(token_count, column_count * cap),
        )

    near_place, near_weights = slot_plan(expert_ids, expert_weights, 0, near_cap)
    far_place, far_weights = slot_plan(group_ids, group_weights, 1, far_cap)
    near_out = jnp.einsum(
        "ts,td->sd",
        near_place.astype(jnp.bfloat16),
        normed,
        preferred_element_type=jnp.float32,
    ).astype(jnp.bfloat16)
    far_out = jnp.einsum(
        "ts,td->sd",
        far_place.astype(jnp.bfloat16),
        group_tokens,
        preferred_element_type=jnp.float32,
    ).astype(jnp.bfloat16)
    near_arrived = lax.all_to_all(
        near_out.reshape(column_count, near_cap, model_width),
        "exp",
        split_axis=0,
        concat_axis=0,
        tiled=True,
    )
    far_arrived = lax.all_to_all(
        far_out.reshape(column_count, far_cap, model_width),
        "exp",
        split_axis=0,
        concat_axis=0,
        tiled=True,
    )
    near_rows = lax.all_gather(near_arrived, "dp", axis=0, tiled=True).reshape(-1, model_width)
    far_rows = far_arrived.reshape(-1, model_width)
    near_terms = shared_block(near_rows, expert_gate[0], expert_up[0], expert_down[0])
    far_terms = shared_block(far_rows, expert_gate[1], expert_up[1], expert_down[1])
    shared_terms = shared_block(group_tokens, shared_gate, shared_up, shared_down)
    near_sum = lax.psum_scatter(
        near_terms.astype(jnp.bfloat16).reshape(row_count, column_count, near_cap, model_width),
        "dp",
        scatter_dimension=0,
        tiled=False,
    )
    far_back = lax.all_to_all(
        far_terms.astype(jnp.bfloat16).reshape(column_count, far_cap, model_width),
        "exp",
        split_axis=0,
        concat_axis=0,
        tiled=True,
    ).reshape(-1, model_width)
    near_back = lax.all_to_all(
        near_sum, "exp", split_axis=0, concat_axis=0, tiled=True
    ).reshape(-1, model_width)

    def combine(slot_weights, rows):
        return jnp.dot(slot_weights.astype(jnp.bfloat16), rows, preferred_element_type=jnp.float32)

    far_part = combine(far_weights, far_back) + shared_terms.astype(
        jnp.bfloat16
    ).astype(jnp.float32)
    far_sum = lax.psum_scatter(
        far_part.astype(jnp.bfloat16).reshape(row_count, tok_rows, model_width),
        "dp",
        scatter_dimension=0,
        tiled=False,
    ).astype(jnp.float32)
    near_part = combine(near_weights, near_back)
    return (residual.astype(jnp.float32) + near_part + far_sum).astype(jnp.bfloat16)


def solution(mesh):
    placed = (
        P(("dp", "exp"), None),
        P(("dp", "exp"), None),
        P(None, ("dp", "exp"), None),
        P(("dp", "exp"), None, None),
        P(("dp", "exp"), None, None),
        P(("dp", "exp"), None),
        P(("dp", "exp")),
        P(("dp", "exp"), None),
        P(),
        P(),
        P("exp", "dp", None),
        P("exp", "dp", None),
        P("exp", "dp", None),
        P("dp", None),
        P("dp", None),
        P("dp", None),
        P(("dp", "exp"), None),
        P(("dp", "exp"), None),
    )
    return jax.shard_map(
        on_device, mesh=mesh, in_specs=placed, out_specs=P(("dp", "exp"), None), check_vma=False
    )
```

```python
import jax
import jax.numpy as jnp
from jax import lax
from jax.sharding import PartitionSpec as P

HEADS = 16
KVH = 4
HD = 128
CAP = 16


NEG_FILL = -1e30
NORM_EPSILON = 1e-06
HIGHEST_PRECISION = lax.Precision.HIGHEST


def tree_reach(parents):
    node_count = parents.shape[-1]
    node_index = jnp.arange(node_count, dtype=jnp.int32)
    linked = (parents[:, :, None] == node_index[None, None, :]).astype(jnp.float32)
    reached = jnp.minimum(linked + jnp.eye(node_count, dtype=jnp.float32)[None], 1.0)
    for rounds in range(max(1, (node_count - 1).bit_length())):
        flags = reached.astype(jnp.bfloat16)
        reached = jnp.minimum(
            jnp.einsum("rij,rjk->rik", flags, flags, preferred_element_type=jnp.float32), 1.0
        )
    return reached


def score_block(query_heads, key_rows, live_mask):
    raw_scores = jnp.einsum(
        "rtgnd,rcgd->rgntc", query_heads, key_rows, preferred_element_type=jnp.float32
    ) * key_rows.shape[-1] ** (-0.5)
    wide_mask = live_mask[:, None, None]
    return (jnp.where(wide_mask, raw_scores, NEG_FILL), wide_mask)


def fold_keys(carry_state, scores, wide_mask, value_rows):
    running_top, running_total, running_sum = carry_state
    fresh_top = jnp.maximum(running_top, jnp.max(scores, axis=-1))
    rescale = jnp.exp(running_top - fresh_top)
    exponents = jnp.where(wide_mask, jnp.exp(scores - fresh_top[..., None]), 0.0)
    weights = exponents.astype(jnp.bfloat16)
    new_total = running_total * rescale + jnp.sum(exponents, axis=-1)
    mixed = jnp.einsum("rgntc,rcgd->rtgnd", weights, value_rows, preferred_element_type=jnp.float32)
    new_sum = running_sum * jnp.transpose(rescale, (0, 3, 1, 2))[..., None] + mixed
    return (fresh_top, new_total, new_sum)


def pool_state(carry_state, query_heads, table_rows, lengths, pieces):
    piece_count = pieces.shape[1]
    request_count, pages_per = table_rows.shape
    page_size = pieces.shape[2]
    key_heads = query_heads.shape[2]
    inside = (table_rows >= 0) & (table_rows < piece_count)
    picked = jnp.clip(table_rows, 0, piece_count - 1)
    picked_pages = pieces[:, picked]
    cache_keys = picked_pages[0].reshape(request_count, pages_per * page_size, key_heads, -1)
    cache_values = picked_pages[1].reshape(request_count, pages_per * page_size, key_heads, -1)
    positions = jnp.arange(pages_per * page_size, dtype=jnp.int32)
    usable = jnp.repeat(inside, page_size, axis=1) & (positions[None, :] < lengths[:, None])
    live_mask = jnp.broadcast_to(
        usable[:, None, :], (request_count, query_heads.shape[1], pages_per * page_size)
    )
    scores, wide_mask = score_block(query_heads, cache_keys, live_mask)
    return fold_keys(carry_state, scores, wide_mask, cache_values)


def blank_state(request_count, draft_nodes, key_heads, group_size, head_size):
    return (
        jnp.full((request_count, key_heads, group_size, draft_nodes), NEG_FILL, jnp.float32),
        jnp.zeros((request_count, key_heads, group_size, draft_nodes), jnp.float32),
        jnp.zeros((request_count, draft_nodes, key_heads, group_size, head_size), jnp.float32),
    )


def expert_block(grouped, gate_rows, upper_rows, down_rows):
    gate_values = jnp.einsum(
        "sekd,efd->sekf", grouped, gate_rows, preferred_element_type=jnp.float32
    )
    upper_values = jnp.einsum(
        "sekd,efd->sekf", grouped, upper_rows, preferred_element_type=jnp.float32
    )
    inner = (jax.nn.silu(gate_values) * upper_values).astype(jnp.bfloat16)
    return jnp.einsum("sekf,efd->sekd", inner, down_rows, preferred_element_type=jnp.float32)


def shared_block(tokens, gate_rows, upper_rows, down_rows):
    unit_count = gate_rows.shape[0]
    both_values = jnp.einsum(
        "td,fd->tf",
        tokens,
        jnp.concatenate([gate_rows, upper_rows], axis=0),
        preferred_element_type=jnp.float32,
    )
    gate_values = both_values[:, :unit_count]
    upper_values = both_values[:, unit_count:]
    inner = (jax.nn.silu(gate_values) * upper_values).astype(jnp.bfloat16)
    return jnp.dot(inner, down_rows, preferred_element_type=jnp.float32)


def on_device(
    hidden,
    queries,
    draft_entries,
    key_pool,
    value_pool,
    page_table,
    cache_len,
    parents,
    out_proj,
    norm_gain,
    expert_gate,
    expert_up,
    expert_down,
    shared_gate,
    shared_up,
    shared_down,
    expert_ids,
    expert_weights,
):
    tok_rows, model_width = hidden.shape
    group_picks = lax.all_gather(
        jnp.concatenate([expert_ids.astype(jnp.float32), expert_weights], axis=1),
        "dp",
        axis=0,
        tiled=True,
    )
    group_picks, queries, draft_entries = lax.optimization_barrier(
        (group_picks, queries, draft_entries)
    )
    local_requests, draft_nodes = parents.shape
    group_size = HEADS // KVH
    query_heads = queries.reshape(local_requests, draft_nodes, KVH, group_size, HD)
    draft_keys = draft_entries[0].reshape(local_requests, draft_nodes, KVH, HD)
    draft_values = draft_entries[1].reshape(local_requests, draft_nodes, KVH, HD)
    reached = tree_reach(parents)
    tree_scores, tree_mask = score_block(query_heads, draft_keys, reached > 0.5)
    tree_state = fold_keys(
        blank_state(local_requests, draft_nodes, KVH, group_size, HD),
        tree_scores,
        tree_mask,
        draft_values,
    )
    both_pools = lax.all_gather(jnp.stack([key_pool, value_pool]), "dp", axis=1, tiled=True)
    final_top, final_total, final_sum = pool_state(
        tree_state,
        query_heads,
        page_table,
        cache_len,
        both_pools,
    )
    attention = (
        (final_sum / jnp.transpose(final_total, (0, 3, 1, 2))[..., None])
        .reshape(tok_rows, queries.shape[1])
        .astype(jnp.bfloat16)
    )
    residual = (
        hidden.astype(jnp.float32)
        + jnp.dot(attention, out_proj, preferred_element_type=jnp.float32)
    ).astype(jnp.bfloat16)
    residual_wide = residual.astype(jnp.float32)
    scale_rows = lax.rsqrt(
        jnp.mean(residual_wide * residual_wide, axis=-1, keepdims=True) + NORM_EPSILON
    )
    normed = (residual_wide * scale_rows * norm_gain.astype(jnp.float32)).astype(jnp.bfloat16)
    column_count = lax.axis_size("exp")
    row_count = lax.axis_size("dp")
    pick_count = expert_ids.shape[1]
    near_cap = CAP
    far_cap = CAP * row_count
    group_tokens = lax.all_gather(normed, "dp", axis=0, tiled=True)
    group_ids = group_picks[:, :pick_count].astype(jnp.int32)
    group_weights = group_picks[:, pick_count:]

    def slot_plan(ids, weights, parity, cap):
        token_count = ids.shape[0]
        picks = ((ids // 2)[:, :, None] == jnp.arange(column_count, dtype=jnp.int32)[None, None, :]) & (
            (ids % 2) == parity
        )[:, :, None]
        member = jnp.any(picks, axis=1)
        token_weight = jnp.sum(jnp.where(picks, weights[:, :, None], 0.0), axis=1)
        earlier = (
            jnp.arange(token_count, dtype=jnp.int32)[:, None]
            > jnp.arange(token_count, dtype=jnp.int32)[None, :]
        ).astype(jnp.bfloat16)
        rank = jnp.dot(
            earlier, member.astype(jnp.bfloat16), preferred_element_type=jnp.float32
        ).astype(jnp.int32)
        place = member[:, :, None] & (
            rank[:, :, None] == jnp.arange(cap, dtype=jnp.int32)[None, None, :]
        )
        slot_weights = jnp.where(place, token_weight[:, :, None], 0.0)
        return (
            place.reshape(token_count, column_count * cap),
            slot_weights.reshape(token_count, column_count * cap),
        )

    near_place, near_weights = slot_plan(expert_ids, expert_weights, 0, near_cap)
    far_place, far_weights = slot_plan(group_ids, group_weights, 1, far_cap)
    near_out = jnp.einsum(
        "ts,td->sd",
        near_place.astype(jnp.bfloat16),
        normed,
        preferred_element_type=jnp.float32,
    ).astype(jnp.bfloat16)
    far_out = jnp.einsum(
        "ts,td->sd",
        far_place.astype(jnp.bfloat16),
        group_tokens,
        preferred_element_type=jnp.float32,
    ).astype(jnp.bfloat16)
    near_arrived = lax.all_to_all(
        near_out.reshape(column_count, near_cap, model_width),
        "exp",
        split_axis=0,
        concat_axis=0,
        tiled=True,
    )
    far_arrived = lax.all_to_all(
        far_out.reshape(column_count, far_cap, model_width),
        "exp",
        split_axis=0,
        concat_axis=0,
        tiled=True,
    )
    near_rows = lax.all_gather(near_arrived, "dp", axis=0, tiled=True).reshape(-1, model_width)
    far_rows = far_arrived.reshape(-1, model_width)
    near_terms = shared_block(near_rows, expert_gate[0], expert_up[0], expert_down[0])
    far_terms = shared_block(far_rows, expert_gate[1], expert_up[1], expert_down[1])
    shared_terms = shared_block(group_tokens, shared_gate, shared_up, shared_down)
    near_sum = lax.psum_scatter(
        near_terms.astype(jnp.bfloat16).reshape(row_count, column_count, near_cap, model_width),
        "dp",
        scatter_dimension=0,
        tiled=False,
    )
    far_back = lax.all_to_all(
        far_terms.astype(jnp.bfloat16).reshape(column_count, far_cap, model_width),
        "exp",
        split_axis=0,
        concat_axis=0,
        tiled=True,
    ).reshape(-1, model_width)
    near_back = lax.all_to_all(
        near_sum, "exp", split_axis=0, concat_axis=0, tiled=True
    ).reshape(-1, model_width)

    def combine(slot_weights, rows):
        return jnp.dot(slot_weights.astype(jnp.bfloat16), rows, preferred_element_type=jnp.float32)

    far_part = combine(far_weights, far_back) + shared_terms.astype(
        jnp.bfloat16
    ).astype(jnp.float32)
    far_sum = lax.psum_scatter(
        far_part.astype(jnp.bfloat16).reshape(row_count, tok_rows, model_width),
        "dp",
        scatter_dimension=0,
        tiled=False,
    ).astype(jnp.float32)
    near_part = combine(near_weights, near_back)
    return (residual.astype(jnp.float32) + near_part + far_sum).astype(jnp.bfloat16)


def solution(mesh):
    placed = (
        P(("dp", "exp"), None),
        P(("dp", "exp"), None),
        P(None, ("dp", "exp"), None),
        P(("dp", "exp"), None, None),
        P(("dp", "exp"), None, None),
        P(("dp", "exp"), None),
        P(("dp", "exp")),
        P(("dp", "exp"), None),
        P(),
        P(),
        P("exp", "dp", None),
        P("exp", "dp", None),
        P("exp", "dp", None),
        P("dp", None),
        P("dp", None),
        P("dp", None),
        P(("dp", "exp"), None),
        P(("dp", "exp"), None),
    )
    return jax.shard_map(
        on_device, mesh=mesh, in_specs=placed, out_specs=P(("dp", "exp"), None), check_vma=False
    )
```

```python
import jax
import jax.numpy as jnp
from jax import lax
from jax.sharding import PartitionSpec as P

HEADS = 16
KVH = 4
HD = 128
CAP = 16


NEG_FILL = -1e30
NORM_EPSILON = 1e-06
HIGHEST_PRECISION = lax.Precision.HIGHEST


def tree_reach(parents):
    node_count = parents.shape[-1]
    node_index = jnp.arange(node_count, dtype=jnp.int32)
    linked = (parents[:, :, None] == node_index[None, None, :]).astype(jnp.float32)
    reached = jnp.minimum(linked + jnp.eye(node_count, dtype=jnp.float32)[None], 1.0)
    def square(rounds, reached):
        flags = reached.astype(jnp.bfloat16)
        return jnp.minimum(
            jnp.einsum("rij,rjk->rik", flags, flags, preferred_element_type=jnp.float32), 1.0
        )

    return lax.fori_loop(0, max(1, (node_count - 1).bit_length()), square, reached)


def score_block(query_heads, key_rows, live_mask):
    raw_scores = jnp.einsum(
        "rtgnd,rcgd->rgntc", query_heads, key_rows, preferred_element_type=jnp.float32
    ) * key_rows.shape[-1] ** (-0.5)
    wide_mask = live_mask[:, None, None]
    return (jnp.where(wide_mask, raw_scores, NEG_FILL), wide_mask)


def fold_keys(carry_state, scores, wide_mask, value_rows):
    running_top, running_total, running_sum = carry_state
    fresh_top = jnp.maximum(running_top, jnp.max(scores, axis=-1))
    rescale = jnp.exp(running_top - fresh_top)
    exponents = jnp.where(wide_mask, jnp.exp(scores - fresh_top[..., None]), 0.0)
    weights = exponents.astype(jnp.bfloat16)
    new_total = running_total * rescale + jnp.sum(exponents, axis=-1)
    mixed = jnp.einsum("rgntc,rcgd->rtgnd", weights, value_rows, preferred_element_type=jnp.float32)
    new_sum = running_sum * jnp.transpose(rescale, (0, 3, 1, 2))[..., None] + mixed
    return (fresh_top, new_total, new_sum)


def pool_state(carry_state, query_heads, table_rows, lengths, pieces):
    piece_count = pieces.shape[1]
    request_count, pages_per = table_rows.shape
    page_size = pieces.shape[2]
    key_heads = query_heads.shape[2]
    inside = (table_rows >= 0) & (table_rows < piece_count)
    picked = jnp.clip(table_rows, 0, piece_count - 1)
    picked_pages = pieces[:, picked]
    cache_keys = picked_pages[0].reshape(request_count, pages_per * page_size, key_heads, -1)
    cache_values = picked_pages[1].reshape(request_count, pages_per * page_size, key_heads, -1)
    positions = jnp.arange(pages_per * page_size, dtype=jnp.int32)
    usable = jnp.repeat(inside, page_size, axis=1) & (positions[None, :] < lengths[:, None])
    live_mask = jnp.broadcast_to(
        usable[:, None, :], (request_count, query_heads.shape[1], pages_per * page_size)
    )
    scores, wide_mask = score_block(query_heads, cache_keys, live_mask)
    return fold_keys(carry_state, scores, wide_mask, cache_values)


def blank_state(request_count, draft_nodes, key_heads, group_size, head_size):
    return (
        jnp.full((request_count, key_heads, group_size, draft_nodes), NEG_FILL, jnp.float32),
        jnp.zeros((request_count, key_heads, group_size, draft_nodes), jnp.float32),
        jnp.zeros((request_count, draft_nodes, key_heads, group_size, head_size), jnp.float32),
    )


def expert_block(grouped, gate_rows, upper_rows, down_rows):
    gate_values = jnp.einsum(
        "sekd,efd->sekf", grouped, gate_rows, preferred_element_type=jnp.float32
    )
    upper_values = jnp.einsum(
        "sekd,efd->sekf", grouped, upper_rows, preferred_element_type=jnp.float32
    )
    inner = (jax.nn.silu(gate_values) * upper_values).astype(jnp.bfloat16)
    return jnp.einsum("sekf,efd->sekd", inner, down_rows, preferred_element_type=jnp.float32)


def shared_block(tokens, gate_rows, upper_rows, down_rows):
    unit_count = gate_rows.shape[0]
    both_values = jnp.einsum(
        "td,fd->tf",
        tokens,
        jnp.concatenate([gate_rows, upper_rows], axis=0),
        preferred_element_type=jnp.float32,
    )
    gate_values = both_values[:, :unit_count]
    upper_values = both_values[:, unit_count:]
    inner = (jax.nn.silu(gate_values) * upper_values).astype(jnp.bfloat16)
    return jnp.dot(inner, down_rows, preferred_element_type=jnp.float32)


def on_device(
    hidden,
    queries,
    draft_entries,
    key_pool,
    value_pool,
    page_table,
    cache_len,
    parents,
    out_proj,
    norm_gain,
    expert_gate,
    expert_up,
    expert_down,
    shared_gate,
    shared_up,
    shared_down,
    expert_ids,
    expert_weights,
):
    tok_rows, model_width = hidden.shape
    group_picks = lax.all_gather(
        jnp.concatenate([expert_ids.astype(jnp.float32), expert_weights], axis=1),
        "dp",
        axis=0,
        tiled=True,
    )
    group_picks, queries, draft_entries = lax.optimization_barrier(
        (group_picks, queries, draft_entries)
    )
    local_requests, draft_nodes = parents.shape
    group_size = HEADS // KVH
    query_heads = queries.reshape(local_requests, draft_nodes, KVH, group_size, HD)
    draft_keys = draft_entries[0].reshape(local_requests, draft_nodes, KVH, HD)
    draft_values = draft_entries[1].reshape(local_requests, draft_nodes, KVH, HD)
    reached = tree_reach(parents)
    tree_scores, tree_mask = score_block(query_heads, draft_keys, reached > 0.5)
    tree_state = fold_keys(
        blank_state(local_requests, draft_nodes, KVH, group_size, HD),
        tree_scores,
        tree_mask,
        draft_values,
    )
    both_pools = lax.all_gather(jnp.stack([key_pool, value_pool]), "dp", axis=1, tiled=True)
    final_top, final_total, final_sum = pool_state(
        tree_state,
        query_heads,
        page_table,
        cache_len,
        both_pools,
    )
    attention = (
        (final_sum / jnp.transpose(final_total, (0, 3, 1, 2))[..., None])
        .reshape(tok_rows, queries.shape[1])
        .astype(jnp.bfloat16)
    )
    residual = (
        hidden.astype(jnp.float32)
        + jnp.dot(attention, out_proj, preferred_element_type=jnp.float32)
    ).astype(jnp.bfloat16)
    residual_wide = residual.astype(jnp.float32)
    scale_rows = lax.rsqrt(
        jnp.mean(residual_wide * residual_wide, axis=-1, keepdims=True) + NORM_EPSILON
    )
    normed = (residual_wide * scale_rows * norm_gain.astype(jnp.float32)).astype(jnp.bfloat16)
    column_count = lax.axis_size("exp")
    row_count = lax.axis_size("dp")
    pick_count = expert_ids.shape[1]
    near_cap = CAP
    far_cap = CAP * row_count
    group_tokens = lax.all_gather(normed, "dp", axis=0, tiled=True)
    group_ids = group_picks[:, :pick_count].astype(jnp.int32)
    group_weights = group_picks[:, pick_count:]

    def slot_plan(ids, weights, parity, cap):
        token_count = ids.shape[0]
        picks = ((ids // 2)[:, :, None] == jnp.arange(column_count, dtype=jnp.int32)[None, None, :]) & (
            (ids % 2) == parity
        )[:, :, None]
        member = jnp.any(picks, axis=1)
        token_weight = jnp.sum(jnp.where(picks, weights[:, :, None], 0.0), axis=1)
        earlier = (
            jnp.arange(token_count, dtype=jnp.int32)[:, None]
            > jnp.arange(token_count, dtype=jnp.int32)[None, :]
        ).astype(jnp.bfloat16)
        rank = jnp.dot(
            earlier, member.astype(jnp.bfloat16), preferred_element_type=jnp.float32
        ).astype(jnp.int32)
        place = member[:, :, None] & (
            rank[:, :, None] == jnp.arange(cap, dtype=jnp.int32)[None, None, :]
        )
        slot_weights = jnp.where(place, token_weight[:, :, None], 0.0)
        return (
            place.reshape(token_count, column_count * cap),
            slot_weights.reshape(token_count, column_count * cap),
        )

    near_place, near_weights = slot_plan(expert_ids, expert_weights, 0, near_cap)
    far_place, far_weights = slot_plan(group_ids, group_weights, 1, far_cap)
    near_out = jnp.einsum(
        "ts,td->sd",
        near_place.astype(jnp.bfloat16),
        normed,
        preferred_element_type=jnp.float32,
    ).astype(jnp.bfloat16)
    far_out = jnp.einsum(
        "ts,td->sd",
        far_place.astype(jnp.bfloat16),
        group_tokens,
        preferred_element_type=jnp.float32,
    ).astype(jnp.bfloat16)
    near_arrived = lax.all_to_all(
        near_out.reshape(column_count, near_cap, model_width),
        "exp",
        split_axis=0,
        concat_axis=0,
        tiled=True,
    )
    far_arrived = lax.all_to_all(
        far_out.reshape(column_count, far_cap, model_width),
        "exp",
        split_axis=0,
        concat_axis=0,
        tiled=True,
    )
    near_rows = lax.all_gather(near_arrived, "dp", axis=0, tiled=True).reshape(-1, model_width)
    far_rows = far_arrived.reshape(-1, model_width)
    near_terms = shared_block(near_rows, expert_gate[0], expert_up[0], expert_down[0])
    far_terms = shared_block(far_rows, expert_gate[1], expert_up[1], expert_down[1])
    shared_terms = shared_block(group_tokens, shared_gate, shared_up, shared_down)
    near_sum = lax.psum_scatter(
        near_terms.astype(jnp.bfloat16).reshape(row_count, column_count, near_cap, model_width),
        "dp",
        scatter_dimension=0,
        tiled=False,
    )
    far_back = lax.all_to_all(
        far_terms.astype(jnp.bfloat16).reshape(column_count, far_cap, model_width),
        "exp",
        split_axis=0,
        concat_axis=0,
        tiled=True,
    ).reshape(-1, model_width)
    near_back = lax.all_to_all(
        near_sum, "exp", split_axis=0, concat_axis=0, tiled=True
    ).reshape(-1, model_width)

    def combine(slot_weights, rows):
        return jnp.dot(slot_weights.astype(jnp.bfloat16), rows, preferred_element_type=jnp.float32)

    far_part = combine(far_weights, far_back) + shared_terms.astype(
        jnp.bfloat16
    ).astype(jnp.float32)
    far_sum = lax.psum_scatter(
        far_part.astype(jnp.bfloat16).reshape(row_count, tok_rows, model_width),
        "dp",
        scatter_dimension=0,
        tiled=False,
    ).astype(jnp.float32)
    near_part = combine(near_weights, near_back)
    return (residual.astype(jnp.float32) + near_part + far_sum).astype(jnp.bfloat16)


def solution(mesh):
    placed = (
        P(("dp", "exp"), None),
        P(("dp", "exp"), None),
        P(None, ("dp", "exp"), None),
        P(("dp", "exp"), None, None),
        P(("dp", "exp"), None, None),
        P(("dp", "exp"), None),
        P(("dp", "exp")),
        P(("dp", "exp"), None),
        P(),
        P(),
        P("exp", "dp", None),
        P("exp", "dp", None),
        P("exp", "dp", None),
        P("dp", None),
        P("dp", None),
        P("dp", None),
        P(("dp", "exp"), None),
        P(("dp", "exp"), None),
    )
    return jax.shard_map(
        on_device, mesh=mesh, in_specs=placed, out_specs=P(("dp", "exp"), None), check_vma=False
    )
```
